32 devices in a mesh: member: 4 (over y, x), space: 8 (over z, core).
Axes of the slice: x: 2, y: 2, z: 4, core: 2. Of those that a mesh axis runs over, the one named last changes fastest.
Arguments:
- ensemble: float32 [64, 128, 2048], P('member', 'space'), may hold values from -6 to 6
- spreading_number: float32 [128, 2048], P('space'), may hold values from 0.05 to 0.2
- zonal_transport_ratio: float32 [128, 2048], P('space'), may hold values from -0.2 to 0.2
- meridional_transport_ratio: float32 [128, 2048], P('space'), may hold values from -0.2 to 0.2
- ocean_mask: int32 [128, 2048], P('space'), may hold values 0 or 1
- obs_loc: int32 [16384], replicated, may hold values from 0 to 262143, as said below
- obs_value: float32 [16384], replicated, may hold values from -6 to 6
- obs_sigma: float32 [16384], replicated, may hold values from 0.3 to 1
- tile_obs: int32 [128, 16, 256], P('space'), may hold values from 0 to 16383, as said below
Outputs:
- analysis: float32 [64, 128, 2048], P('member', 'space')
The draws below stay inside these ranges and needn't reach their ends.
Inputs may be any that keep to these rules, and one draw needn't show every extreme that they name: `obs_loc`: observation j lies in grid rows (j // 2048) * 16 to (j // 2048 + 1) * 16 - 1. `tile_obs`: the observations named for a tile in grid row r have indices from (r // 16 - 1) * 2048 to (r // 16 + 2) * 2048 - 1; repeats may occur.
All inputs are finite; a program needn't handle non-finite values. No bound on the sum of `ocean_mask` on one device may be relied on, other than what follows from the above.
Results may differ from the reference program's by a relative error of at most 0.0003.
Values sent between devices are 32-bit elements; how exact they have to be, the bound alone decides.
No kernel may reach another device: no remote copies, remote signals or barrier semaphores. Data moves between devices by JAX's collectives and lax.ppermute only.
A program may use at most 64 MiB of HBM per device.

```python
import math
import jax
import jax.numpy as jnp
from jax import lax

MEMBERS = 64
CY = 16
NX = 2048
NY = 128
TILE_COLS = 128
OBS_DEV = 2048
OBS_ALL = 16384
OBS_TILE = 256
LOC_RADIUS = 96
NS_ITERS = 6


def draw_obs_loc(key, part):
    subkeys = jax.random.split(key, 2)
    obs_index = jnp.arange(OBS_ALL, dtype=jnp.int32)
    owner_tile = obs_index // OBS_DEV
    local_index = obs_index % OBS_DEV
    jitter = max(NX // OBS_DEV, 1)
    grid_row = owner_tile * CY + jax.random.randint(subkeys[0], (OBS_ALL,), 0, CY)
    grid_col = local_index * NX // OBS_DEV + jax.random.randint(subkeys[1], (OBS_ALL,), 0, jitter)
    return (grid_row * NX + grid_col).astype(jnp.int32)


def draw_tile_obs(key, part):
    subkeys = jax.random.split(key, 2)
    out_shape = (NY, NX // TILE_COLS, OBS_TILE)
    grid_row = jnp.arange(NY, dtype=jnp.int32).reshape(NY, 1, 1)
    tile_col = jnp.arange(NX // TILE_COLS, dtype=jnp.int32).reshape(1, NX // TILE_COLS, 1)
    home_tile = grid_row // CY
    near_tile = jnp.clip(home_tile + jax.random.randint(subkeys[0], out_shape, -1, 2), 0, NY // CY - 1)
    col_span = TILE_COLS * OBS_DEV // NX
    offset = jax.random.randint(subkeys[1], out_shape, -col_span, 2 * col_span)
    local_index = (tile_col * col_span + offset) % OBS_DEV
    return (near_tile * OBS_DEV + local_index).astype(jnp.int32)


def plant(array, stream_key, least, largest):
    place = [jax.random.randint(jax.random.fold_in(stream_key, axis), (), 0, length) for axis, length in enumerate(array.shape)]
    longest = array.shape.index(max(array.shape))
    next_to = place[:longest] + [(place[longest] + 1) % array.shape[longest]] + place[longest + 1:]
    return array.at[tuple(place)].set(least).at[tuple(next_to)].set(largest)


def level_of(key, shape, cuts, least, high):
    gain, own = 1.0, jax.random.fold_in(key, 6)
    for dim, parts in cuts:
        draws = jnp.exp(jax.random.uniform(jax.random.fold_in(own, dim), (parts,), jnp.float32, least / len(cuts), high / len(cuts)))
        gain = gain * jnp.repeat(draws, shape[dim] // parts).reshape([-1 if axis == dim else 1 for axis in range(len(shape))])
    return gain


def noise(stream_key, shape, width, reach, cuts=(), held_as=jnp.bfloat16):
    level = level_of(stream_key, shape, cuts, -0.22, 0.18) if cuts else 1.0
    values = jax.random.normal(stream_key, shape, jnp.float32) * width * level
    return jnp.minimum(jnp.maximum(values, -reach), reach).astype(held_as)


def setup_inputs(seed: int = 0) -> dict:
    arg_keys = jax.random.split(jax.random.key(seed), 10)
    return {
        "ensemble": noise(arg_keys[0], (MEMBERS, NY, NX), 1.0, 6.0, ((0, 4), (1, 8)), jnp.float32),
        "spreading_number": jnp.clip(0.05 + 0.15 * jax.random.uniform(arg_keys[1], (NY, NX), jnp.float32) ** level_of(arg_keys[1], (NY, NX), ((0, 8),), -0.2, 0.2), 0.05, 0.2),
        "zonal_transport_ratio": jnp.clip(jax.random.uniform(arg_keys[2], (NY, NX), jnp.float32, -0.2, 0.2) * level_of(arg_keys[2], (NY, NX), ((0, 8),), -0.4, 0.0), -0.2, 0.2),
        "meridional_transport_ratio": jnp.clip(jax.random.uniform(arg_keys[3], (NY, NX), jnp.float32, -0.2, 0.2) * level_of(arg_keys[3], (NY, NX), ((0, 8),), -0.4, 0.0), -0.2, 0.2),
        "ocean_mask": plant((jax.random.randint(arg_keys[4], (NY, NX), 0, 10) < 7).astype(jnp.int32), jax.random.fold_in(arg_keys[4], 1), 0, 1),
        "obs_loc": draw_obs_loc(jax.random.fold_in(arg_keys[9], 71), 0),
        "obs_value": noise(arg_keys[6], (OBS_ALL,), 1.0, 6.0, (), jnp.float32),
        "obs_sigma": jnp.clip(jnp.exp(jax.random.uniform(arg_keys[7], (OBS_ALL,), jnp.float32, math.log(0.3), math.log(1.0))), 0.3, 1.0),
        "tile_obs": draw_tile_obs(jax.random.fold_in(arg_keys[9], 71), 0),
    }


highest = lax.Precision.HIGHEST

def propagate_prior_state(haloed_state_grid, spreading_number, zonal_transport_ratio, meridional_transport_ratio, liquid_cell_flags):
    centre = haloed_state_grid[:, 1:-1, :]
    northern = haloed_state_grid[:, 2:, :]
    southern = haloed_state_grid[:, :-2, :]
    eastern = jnp.roll(centre, -1, axis=2)
    western = jnp.roll(centre, 1, axis=2)
    laplace = northern + southern + eastern + western - 4.0 * centre
    advect = zonal_transport_ratio * (eastern - western) * 0.5 + meridional_transport_ratio * (northern - southern) * 0.5
    return liquid_cell_flags * (centre + spreading_number * laplace - advect)

def analyze(ensemble_block, anomalies, means, window_picks, global_picks, obs_loc, obs_value, obs_sigma, row_first, col_first, grid_cols):
    members, block_rows, block_cols = ensemble_block.shape
    tile_cols = block_cols // TILE_COLS
    tile_count = block_rows * tile_cols
    window_flat = window_picks.reshape(tile_count, -1)
    global_flat = global_picks.reshape(tile_count, -1)
    chosen = jnp.take(anomalies, window_flat, axis=1)
    chosen_mean = jnp.take(means, window_flat)
    location = jnp.take(obs_loc, global_flat)
    obs_row = location // grid_cols
    obs_col = location % grid_cols
    zero_grid = jnp.zeros((block_rows, tile_cols), jnp.int32)
    tile_row = (row_first + jnp.arange(block_rows, dtype=jnp.int32)[:, None] + zero_grid).reshape(tile_count, 1)
    tile_start = (col_first + TILE_COLS * jnp.arange(tile_cols, dtype=jnp.int32)[None, :] + zero_grid).reshape(tile_count, 1)
    row_gap = (obs_row - tile_row).astype(jnp.float32)
    col_twice = 2 * obs_col - 2 * tile_start - (TILE_COLS - 1)
    col_twice = (col_twice + grid_cols) % (2 * grid_cols) - grid_cols
    col_gap = 0.5 * col_twice.astype(jnp.float32)
    distance = row_gap * row_gap + col_gap * col_gap
    tapering = jnp.exp(-distance / (2.0 * LOC_RADIUS * LOC_RADIUS))
    sigma_sel = jnp.take(obs_sigma, global_flat)
    obs_weight = tapering / (sigma_sel * sigma_sel)
    innovation = jnp.take(obs_value, global_flat) - chosen_mean
    weighted = chosen * obs_weight[None]
    gram_matrix = jnp.einsum('knl,jnl->nkj', weighted, chosen, precision=highest)
    identity = jnp.eye(members, dtype=jnp.float32)
    system = gram_matrix + (members - 1.0) * identity
    frob_norm = jnp.sqrt(lax.optimization_barrier(jnp.sum(system * system, axis=(1, 2))))
    iterate = system / frob_norm[:, None, None]
    inverse_root = jnp.broadcast_to(identity, system.shape)
    for sweep_index in range(NS_ITERS):
        factor = 1.5 * identity - 0.5 * jnp.einsum('nij,njk->nik', inverse_root, iterate, precision=highest)
        iterate = jnp.einsum('nij,njk->nik', iterate, factor, precision=highest)
        inverse_root = jnp.einsum('nij,njk->nik', factor, inverse_root, precision=highest)
    forcing = jnp.einsum('knl,nl->nk', chosen, obs_weight * innovation, precision=highest)
    half_step = jnp.einsum('nkj,nj->nk', inverse_root, forcing, precision=highest)
    mean_weight = jnp.einsum('nkj,nj->nk', inverse_root, half_step, precision=highest) / frob_norm[:, None]
    transform = jnp.sqrt(members - 1.0) * inverse_root / jnp.sqrt(frob_norm)[:, None, None] + mean_weight[:, :, None]
    tile_cells = ensemble_block.reshape(members, tile_count, TILE_COLS)
    centre_mean = lax.optimization_barrier(jnp.mean(tile_cells, axis=0))
    spread = tile_cells - centre_mean
    analysis = centre_mean + jnp.einsum('jnt,njk->knt', spread, transform, precision=highest)
    return analysis.reshape(members, block_rows, block_cols)

def reference(ensemble, spreading_number, zonal_transport_ratio, meridional_transport_ratio, ocean_mask, obs_loc, obs_value, obs_sigma, tile_obs):
    liquid_cell_flags = ocean_mask.astype(jnp.float32)
    level_state_grid = liquid_cell_flags * ensemble
    for prior_step_tally in range(2):
        haloed_state_grid = jnp.pad(level_state_grid, ((0, 0), (1, 1), (0, 0)))
        level_state_grid = propagate_prior_state(haloed_state_grid, spreading_number, zonal_transport_ratio, meridional_transport_ratio, liquid_cell_flags)
    members = level_state_grid.shape[0]
    observed = jnp.take(level_state_grid.reshape(members, NY * NX), obs_loc, axis=1)
    obs_mean = lax.optimization_barrier(jnp.mean(observed, axis=0))
    obs_anom = observed - obs_mean
    band_count = NY // CY
    blocks = level_state_grid.reshape(members, band_count, CY, NX).transpose(1, 0, 2, 3)
    all_picks = tile_obs.reshape(band_count, CY, NX // TILE_COLS, OBS_TILE)

    def one_block(operands):
        ensemble_block, chosen_picks, block_index = operands
        return analyze(ensemble_block, obs_anom, obs_mean, chosen_picks, chosen_picks, obs_loc, obs_value, obs_sigma, block_index * CY, 0, NX)
    result = lax.map(one_block, (blocks, all_picks, jnp.arange(band_count, dtype=jnp.int32)))
    return result.transpose(1, 0, 2, 3).reshape(members, NY, NX)
```

```python
import functools
import jax
import jax.numpy as jnp
from jax import lax
from jax.experimental import pallas as pl
from jax.experimental.pallas import tpu as pltpu
from jax.sharding import PartitionSpec as P

TILE_COLS = 128
OBS_TILE = 256
LOC_RADIUS = 96
NS_ITERS = 6


highest = lax.Precision.HIGHEST


def padded(cells, sides, width):
    for axis, dim in sides:
        count = lax.axis_size(axis)
        ends = count - 1
        head = lax.slice_in_dim(cells, 0, width, axis=dim)
        tail = lax.slice_in_dim(cells, cells.shape[dim] - width, cells.shape[dim], axis=dim)
        cells = jnp.concatenate(
            [
                lax.ppermute(tail, axis, [(i, (i + 1) % count) for i in range(ends)]),
                cells,
                lax.ppermute(head, axis, [((i + 1) % count, i) for i in range(ends)]),
            ],
            axis=dim,
        )
    return cells


def propagate_prior_state(
    haloed_state_grid,
    spreading_number,
    zonal_transport_ratio,
    meridional_transport_ratio,
    liquid_cell_flags,
):
    centre = haloed_state_grid[:, 1:-1, :]
    northern = haloed_state_grid[:, 2:, :]
    southern = haloed_state_grid[:, :-2, :]
    eastern = jnp.roll(centre, -1, axis=2)
    western = jnp.roll(centre, 1, axis=2)
    laplace = northern + southern + eastern + western - 4.0 * centre
    advect = (
        zonal_transport_ratio * (eastern - western) * 0.5
        + meridional_transport_ratio * (northern - southern) * 0.5
    )
    return liquid_cell_flags * (centre + spreading_number * laplace - advect)


def gram_kernel(picks_ref, meta_ref, table_ref, out_ref, buf_ref, *, tb, tile_cols, grid_cols, members):
    step = pl.program_id(0)
    base = step * (tb * OBS_TILE)

    def gather(j, carry):
        for u in range(8):
            i = j * 8 + u
            idx = picks_ref[base + i]
            buf_ref[pl.ds(i, 1), :] = table_ref[pl.ds(idx, 1), :]
        return carry

    lax.fori_loop(0, tb * OBS_TILE // 8, gather, 0)
    row_first = meta_ref[0]
    width = buf_ref.shape[1]
    lane = lax.broadcasted_iota(jnp.int32, (OBS_TILE, width), 1)
    for t in range(tb):
        n = step * tb + t
        tile_row = jnp.full((OBS_TILE, 1), row_first + n // tile_cols, jnp.int32).astype(jnp.float32)
        tile_start = jnp.full((OBS_TILE, 1), TILE_COLS * (n % tile_cols), jnp.int32).astype(jnp.float32)
        blk = buf_ref[pl.ds(t * OBS_TILE, OBS_TILE), :]
        sig = blk[:, members + 1 : members + 2]
        orow = blk[:, members + 2 : members + 3]
        ocol = blk[:, members + 3 : members + 4]
        row_gap = orow - tile_row
        col_twice = 2.0 * ocol - 2.0 * tile_start - float(TILE_COLS - 1)
        col_twice = jnp.where(col_twice >= grid_cols, col_twice - 2.0 * grid_cols, col_twice)
        col_twice = jnp.where(col_twice < -grid_cols, col_twice + 2.0 * grid_cols, col_twice)
        col_gap = 0.5 * col_twice
        distance = row_gap * row_gap + col_gap * col_gap
        tapering = jnp.exp(-distance / (2.0 * LOC_RADIUS * LOC_RADIUS))
        weight = tapering / (sig * sig)
        rhs = jnp.where(lane <= members, blk, 0.0) * weight
        out_ref[t] = lax.dot_general(
            blk[:, :members],
            rhs,
            (((0,), (0,)), ((), ())),
            precision=highest,
            preferred_element_type=jnp.float32,
        )


def gram_and_forcing(table, picks, row_first, tile_cols, grid_cols, members):
    tile_count = picks.shape[0]
    tb = 8 if tile_count % 8 == 0 else 1
    window, width = table.shape
    kernel = functools.partial(
        gram_kernel, tb=tb, tile_cols=tile_cols, grid_cols=grid_cols, members=members
    )
    meta = jnp.reshape(row_first, (1,)).astype(jnp.int32)
    return pl.pallas_call(
        kernel,
        grid_spec=pltpu.PrefetchScalarGridSpec(
            num_scalar_prefetch=2,
            grid=(tile_count // tb,),
            in_specs=[pl.BlockSpec((window, width), lambda s, p, m: (0, 0))],
            out_specs=pl.BlockSpec((tb, members, width), lambda s, p, m: (s, 0, 0)),
            scratch_shapes=[pltpu.VMEM((tb * OBS_TILE, width), jnp.float32)],
        ),
        out_shape=jax.ShapeDtypeStruct((tile_count, members, width), jnp.float32),
    )(picks.reshape(-1), meta, table)


def analyze(ensemble_block, table, picks, row_first, grid_cols):
    members, block_rows, block_cols = ensemble_block.shape
    tile_cols = block_cols // TILE_COLS
    tile_count = block_rows * tile_cols
    moments = gram_and_forcing(
        table, picks.reshape(tile_count, -1), row_first, tile_cols, grid_cols, members
    )
    gram_matrix = moments[:, :, :members]
    forcing = moments[:, :, members]
    identity = jnp.eye(members, dtype=jnp.float32)
    system = gram_matrix + (members - 1.0) * identity
    frob_norm = jnp.sqrt(jnp.sum(system * system, axis=(1, 2)))
    iterate = system / frob_norm[:, None, None]
    inverse_root = jnp.broadcast_to(identity, system.shape)
    for sweep_index in range(NS_ITERS):
        factor = 1.5 * identity - 0.5 * jnp.einsum(
            "nij,njk->nik", inverse_root, iterate, precision=highest
        )
        iterate = jnp.einsum("nij,njk->nik", iterate, factor, precision=highest)
        inverse_root = jnp.einsum("nij,njk->nik", factor, inverse_root, precision=highest)
    half_step = jnp.einsum("nkj,nj->nk", inverse_root, forcing, precision=highest)
    mean_weight = (
        jnp.einsum("nkj,nj->nk", inverse_root, half_step, precision=highest) / frob_norm[:, None]
    )
    transform = (
        jnp.sqrt(members - 1.0) * inverse_root / jnp.sqrt(frob_norm)[:, None, None]
        + mean_weight[:, :, None]
    )
    tile_cells = ensemble_block.reshape(members, tile_count, TILE_COLS)
    centre_mean = jnp.mean(tile_cells, axis=0)
    spread = tile_cells - centre_mean
    analysis = centre_mean + jnp.einsum("jnt,njk->knt", spread, transform, precision=highest)
    return analysis.reshape(members, block_rows, block_cols)


def on_device(
    ensemble,
    spreading_number,
    zonal_transport_ratio,
    meridional_transport_ratio,
    ocean_mask,
    obs_loc,
    obs_value,
    obs_sigma,
    tile_obs,
):
    mem_dev, row_count, col_count = ensemble.shape
    liquid_cell_flags = ocean_mask.astype(jnp.float32)
    level_state_grid = liquid_cell_flags * ensemble
    for prior_step_tally in range(2):
        haloed_state_grid = padded(level_state_grid, (("space", 1),), 1)
        level_state_grid = propagate_prior_state(
            haloed_state_grid,
            spreading_number,
            zonal_transport_ratio,
            meridional_transport_ratio,
            liquid_cell_flags,
        )
    space_index = lax.axis_index("space")
    member_index = lax.axis_index("member")
    obs_dev = obs_loc.shape[0] // lax.axis_size("space")
    flattened = level_state_grid.reshape(mem_dev, row_count * col_count)
    own_loc = lax.dynamic_slice_in_dim(obs_loc, space_index * obs_dev, obs_dev) - space_index * (
        row_count * col_count
    )
    own_obs = jnp.take(flattened, own_loc, axis=1)
    rimmed = padded(own_obs, (("space", 1),), obs_dev)
    window = lax.all_gather(rimmed, "member", axis=0, tiled=True)
    members = window.shape[0]
    window_mean = jnp.mean(window, axis=0)
    window_anom = window - window_mean
    window_len = window.shape[1]

    def window_of(values, fill):
        rim = jnp.full((obs_dev,), fill, values.dtype)
        return lax.dynamic_slice_in_dim(
            jnp.concatenate([rim, values, rim]), space_index * obs_dev, window_len
        )

    window_loc = window_of(obs_loc, 0)
    innovation = window_of(obs_value, 0.0) - window_mean
    width = -(-(members + 4) // 128) * 128
    table = jnp.concatenate(
        [
            window_anom.T,
            innovation[:, None],
            window_of(obs_sigma, 1.0)[:, None],
            (window_loc // col_count).astype(jnp.float32)[:, None],
            (window_loc % col_count).astype(jnp.float32)[:, None],
            jnp.zeros((window_len, width - members - 4), jnp.float32),
        ],
        axis=1,
    )
    first_obs = (space_index - 1) * obs_dev
    cell_block = lax.all_to_all(level_state_grid, "member", split_axis=1, concat_axis=0, tiled=True)
    block_rows = cell_block.shape[1]
    tile_picks = lax.dynamic_slice_in_dim(tile_obs, member_index * block_rows, block_rows, 0)
    local_picks = jnp.clip(tile_picks - first_obs, 0, window_len - 1)
    row_first = space_index * row_count + member_index * block_rows
    updated = analyze(cell_block, table, local_picks, row_first, col_count)
    result = lax.all_to_all(updated, "member", split_axis=0, concat_axis=1, tiled=True)
    return result


def solution(mesh):
    in_specs = (
        P("member", "space", None),
        P("space", None),
        P("space", None),
        P("space", None),
        P("space", None),
        P(),
        P(),
        P(),
        P("space", None, None),
    )
    out_specs = P("member", "space", None)
    return jax.shard_map(
        on_device, mesh=mesh, in_specs=in_specs, out_specs=out_specs, check_vma=False
    )
```

```python
import functools
import jax
import jax.numpy as jnp
from jax import lax
from jax.experimental import pallas as pl
from jax.experimental.pallas import tpu as pltpu
from jax.sharding import PartitionSpec as P

TILE_COLS = 128
OBS_TILE = 256
LOC_RADIUS = 96
NS_ITERS = 6


highest = lax.Precision.HIGHEST


def padded(cells, sides, width):
    for axis, dim in sides:
        count = lax.axis_size(axis)
        ends = count - 1
        head = lax.slice_in_dim(cells, 0, width, axis=dim)
        tail = lax.slice_in_dim(cells, cells.shape[dim] - width, cells.shape[dim], axis=dim)
        cells = jnp.concatenate(
            [
                lax.ppermute(tail, axis, [(i, (i + 1) % count) for i in range(ends)]),
                cells,
                lax.ppermute(head, axis, [((i + 1) % count, i) for i in range(ends)]),
            ],
            axis=dim,
        )
    return cells


def propagate_prior_state(
    haloed_state_grid,
    spreading_number,
    zonal_transport_ratio,
    meridional_transport_ratio,
    liquid_cell_flags,
):
    centre = haloed_state_grid[:, 1:-1, :]
    northern = haloed_state_grid[:, 2:, :]
    southern = haloed_state_grid[:, :-2, :]
    eastern = jnp.roll(centre, -1, axis=2)
    western = jnp.roll(centre, 1, axis=2)
    laplace = northern + southern + eastern + western - 4.0 * centre
    advect = (
        zonal_transport_ratio * (eastern - western) * 0.5
        + meridional_transport_ratio * (northern - southern) * 0.5
    )
    return liquid_cell_flags * (centre + spreading_number * laplace - advect)


def gram_kernel(picks_ref, meta_ref, table_ref, out_ref, buf_ref, *, tb, tile_cols, grid_cols, members):
    step = pl.program_id(0)
    base = step * (tb * OBS_TILE)

    def gather(j, carry):
        for u in range(8):
            i = j * 8 + u
            idx = picks_ref[base + i]
            buf_ref[pl.ds(i, 1), :] = table_ref[pl.ds(idx, 1), :]
        return carry

    lax.fori_loop(0, tb * OBS_TILE // 8, gather, 0)
    row_first = meta_ref[0]
    width = buf_ref.shape[1]
    lane = lax.broadcasted_iota(jnp.int32, (OBS_TILE, width), 1)
    for t in range(tb):
        n = step * tb + t
        tile_row = jnp.full((OBS_TILE, 1), row_first + n // tile_cols, jnp.int32).astype(jnp.float32)
        tile_start = jnp.full((OBS_TILE, 1), TILE_COLS * (n % tile_cols), jnp.int32).astype(jnp.float32)
        blk = buf_ref[pl.ds(t * OBS_TILE, OBS_TILE), :]
        sig = blk[:, members + 1 : members + 2]
        orow = blk[:, members + 2 : members + 3]
        ocol = blk[:, members + 3 : members + 4]
        row_gap = orow - tile_row
        col_twice = 2.0 * ocol - 2.0 * tile_start - float(TILE_COLS - 1)
        col_twice = jnp.where(col_twice >= grid_cols, col_twice - 2.0 * grid_cols, col_twice)
        col_twice = jnp.where(col_twice < -grid_cols, col_twice + 2.0 * grid_cols, col_twice)
        col_gap = 0.5 * col_twice
        distance = row_gap * row_gap + col_gap * col_gap
        tapering = jnp.exp(-distance / (2.0 * LOC_RADIUS * LOC_RADIUS))
        weight = tapering / (sig * sig)
        rhs = jnp.where(lane <= members, blk, 0.0) * weight
        out_ref[t] = lax.dot_general(
            blk[:, :members],
            rhs,
            (((0,), (0,)), ((), ())),
            precision=highest,
            preferred_element_type=jnp.float32,
        )


def gram_and_forcing(table, picks, row_first, tile_cols, grid_cols, members):
    tile_count = picks.shape[0]
    tb = 8 if tile_count % 8 == 0 else 1
    window, width = table.shape
    kernel = functools.partial(
        gram_kernel, tb=tb, tile_cols=tile_cols, grid_cols=grid_cols, members=members
    )
    meta = jnp.reshape(row_first, (1,)).astype(jnp.int32)
    return pl.pallas_call(
        kernel,
        grid_spec=pltpu.PrefetchScalarGridSpec(
            num_scalar_prefetch=2,
            grid=(tile_count // tb,),
            in_specs=[pl.BlockSpec((window, width), lambda s, p, m: (0, 0))],
            out_specs=pl.BlockSpec((tb, members, width), lambda s, p, m: (s, 0, 0)),
            scratch_shapes=[pltpu.VMEM((tb * OBS_TILE, width), jnp.float32)],
        ),
        out_shape=jax.ShapeDtypeStruct((tile_count, members, width), jnp.float32),
    )(picks.reshape(-1), meta, table)


def analyze(ensemble_block, table, picks, row_first, grid_cols):
    members, block_rows, block_cols = ensemble_block.shape
    tile_cols = block_cols // TILE_COLS
    tile_count = block_rows * tile_cols
    moments = gram_and_forcing(
        table, picks.reshape(tile_count, -1), row_first, tile_cols, grid_cols, members
    )
    gram_matrix = moments[:, :, :members]
    forcing = moments[:, :, members]
    identity = jnp.eye(members, dtype=jnp.float32)
    system = gram_matrix + (members - 1.0) * identity
    frob_norm = jnp.sqrt(jnp.sum(system * system, axis=(1, 2)))
    iterate = system / frob_norm[:, None, None]
    factor = 1.5 * identity - 0.5 * iterate
    iterate = jnp.einsum("nij,njk->nik", iterate, factor, precision=highest)
    inverse_root = factor
    for sweep_index in range(1, NS_ITERS):
        factor = 1.5 * identity - 0.5 * jnp.einsum(
            "nij,njk->nik", inverse_root, iterate, precision=highest
        )
        iterate = jnp.einsum("nij,njk->nik", iterate, factor, precision=highest)
        inverse_root = jnp.einsum("nij,njk->nik", factor, inverse_root, precision=highest)
    half_step = jnp.einsum("nkj,nj->nk", inverse_root, forcing, precision=highest)
    mean_weight = (
        jnp.einsum("nkj,nj->nk", inverse_root, half_step, precision=highest) / frob_norm[:, None]
    )
    transform = (
        jnp.sqrt(members - 1.0) * inverse_root / jnp.sqrt(frob_norm)[:, None, None]
        + mean_weight[:, :, None]
    )
    tile_cells = ensemble_block.reshape(members, tile_count, TILE_COLS)
    centre_mean = jnp.mean(tile_cells, axis=0)
    spread = tile_cells - centre_mean
    analysis = centre_mean + jnp.einsum("jnt,njk->knt", spread, transform, precision=highest)
    return analysis.reshape(members, block_rows, block_cols)


def on_device(
    ensemble,
    spreading_number,
    zonal_transport_ratio,
    meridional_transport_ratio,
    ocean_mask,
    obs_loc,
    obs_value,
    obs_sigma,
    tile_obs,
):
    mem_dev, row_count, col_count = ensemble.shape
    liquid_cell_flags = ocean_mask.astype(jnp.float32)
    level_state_grid = liquid_cell_flags * ensemble
    for prior_step_tally in range(2):
        haloed_state_grid = padded(level_state_grid, (("space", 1),), 1)
        level_state_grid = propagate_prior_state(
            haloed_state_grid,
            spreading_number,
            zonal_transport_ratio,
            meridional_transport_ratio,
            liquid_cell_flags,
        )
    space_index = lax.axis_index("space")
    member_index = lax.axis_index("member")
    obs_dev = obs_loc.shape[0] // lax.axis_size("space")
    own_loc = lax.dynamic_slice_in_dim(obs_loc, space_index * obs_dev, obs_dev) - space_index * (
        row_count * col_count
    )
    own_obs = level_state_grid[:, own_loc // col_count, own_loc % col_count]
    rimmed = padded(own_obs, (("space", 1),), obs_dev)
    window = lax.all_gather(rimmed, "member", axis=0, tiled=True)
    members = window.shape[0]
    window_mean = jnp.mean(window, axis=0)
    window_anom = window - window_mean
    window_len = window.shape[1]

    def window_of(values, fill):
        rim = jnp.full((obs_dev,), fill, values.dtype)
        return lax.dynamic_slice_in_dim(
            jnp.concatenate([rim, values, rim]), space_index * obs_dev, window_len
        )

    window_loc = window_of(obs_loc, 0)
    innovation = window_of(obs_value, 0.0) - window_mean
    width = -(-(members + 4) // 128) * 128
    table = jnp.concatenate(
        [
            window_anom,
            innovation[None],
            window_of(obs_sigma, 1.0)[None],
            (window_loc // col_count).astype(jnp.float32)[None],
            (window_loc % col_count).astype(jnp.float32)[None],
            jnp.zeros((width - members - 4, window_len), jnp.float32),
        ],
        axis=0,
    ).T
    first_obs = (space_index - 1) * obs_dev
    cell_block = lax.all_to_all(level_state_grid, "member", split_axis=1, concat_axis=0, tiled=True)
    block_rows = cell_block.shape[1]
    tile_picks = lax.dynamic_slice_in_dim(tile_obs, member_index * block_rows, block_rows, 0)
    local_picks = jnp.clip(tile_picks - first_obs, 0, window_len - 1)
    row_first = space_index * row_count + member_index * block_rows
    updated = analyze(cell_block, table, local_picks, row_first, col_count)
    result = lax.all_to_all(updated, "member", split_axis=0, concat_axis=1, tiled=True)
    return result


def solution(mesh):
    in_specs = (
        P("member", "space", None),
        P("space", None),
        P("space", None),
        P("space", None),
        P("space", None),
        P(),
        P(),
        P(),
        P("space", None, None),
    )
    out_specs = P("member", "space", None)
    return jax.shard_map(
        on_device, mesh=mesh, in_specs=in_specs, out_specs=out_specs, check_vma=False
    )
```

```python
import functools
import jax
import jax.numpy as jnp
from jax import lax
from jax.experimental import pallas as pl
from jax.experimental.pallas import tpu as pltpu
from jax.sharding import PartitionSpec as P

TILE_COLS = 128
OBS_TILE = 256
LOC_RADIUS = 96
NS_ITERS = 6


highest = lax.Precision.HIGHEST


def padded(cells, sides, width):
    for axis, dim in sides:
        count = lax.axis_size(axis)
        ends = count - 1
        head = lax.slice_in_dim(cells, 0, width, axis=dim)
        tail = lax.slice_in_dim(cells, cells.shape[dim] - width, cells.shape[dim], axis=dim)
        cells = jnp.concatenate(
            [
                lax.ppermute(tail, axis, [(i, (i + 1) % count) for i in range(ends)]),
                cells,
                lax.ppermute(head, axis, [((i + 1) % count, i) for i in range(ends)]),
            ],
            axis=dim,
        )
    return cells


def propagate_prior_state(
    haloed_state_grid,
    spreading_number,
    zonal_transport_ratio,
    meridional_transport_ratio,
    liquid_cell_flags,
):
    centre = haloed_state_grid[:, 1:-1, :]
    northern = haloed_state_grid[:, 2:, :]
    southern = haloed_state_grid[:, :-2, :]
    eastern = jnp.roll(centre, -1, axis=2)
    western = jnp.roll(centre, 1, axis=2)
    laplace = northern + southern + eastern + western - 4.0 * centre
    advect = (
        zonal_transport_ratio * (eastern - western) * 0.5
        + meridional_transport_ratio * (northern - southern) * 0.5
    )
    return liquid_cell_flags * (centre + spreading_number * laplace - advect)


def gram_kernel(
    picks_ref, meta_ref, window_ref, aux_ref, out_ref, table_ref, buf_ref, *, tb, tile_cols, grid_cols, members
):
    step = pl.program_id(0)
    base = step * (tb * OBS_TILE)
    width = table_ref.shape[1]

    @pl.when(step == 0)
    def _():
        def build(c, carry):
            start = pl.multiple_of(c * 128, 128)
            values = window_ref[:, pl.ds(start, 128)]
            mean = jnp.mean(values, axis=0, keepdims=True)
            extra = aux_ref[:, pl.ds(start, 128)]
            first = lax.broadcasted_iota(jnp.int32, extra.shape, 0) == 0
            extra = jnp.where(first, extra - mean, extra)
            rows = jnp.concatenate(
                [values - mean, extra, jnp.zeros((width - members - 8, 128), jnp.float32)], axis=0
            )
            table_ref[pl.ds(start, 128), :] = rows.T
            return carry

        lax.fori_loop(0, table_ref.shape[0] // 128, build, 0)


    def gather(j, carry):
        for u in range(8):
            i = j * 8 + u
            idx = picks_ref[base + i]
            buf_ref[pl.ds(i, 1), :] = table_ref[pl.ds(idx, 1), :]
        return carry

    lax.fori_loop(0, tb * OBS_TILE // 8, gather, 0)
    row_first = meta_ref[0]
    lane = lax.broadcasted_iota(jnp.int32, (OBS_TILE, width), 1)
    for t in range(tb):
        n = step * tb + t
        tile_row = jnp.full((OBS_TILE, 1), row_first + n // tile_cols, jnp.int32).astype(jnp.float32)
        tile_start = jnp.full((OBS_TILE, 1), TILE_COLS * (n % tile_cols), jnp.int32).astype(jnp.float32)
        blk = buf_ref[pl.ds(t * OBS_TILE, OBS_TILE), :]
        sig = blk[:, members + 1 : members + 2]
        orow = blk[:, members + 2 : members + 3]
        ocol = blk[:, members + 3 : members + 4]
        row_gap = orow - tile_row
        col_twice = 2.0 * ocol - 2.0 * tile_start - float(TILE_COLS - 1)
        col_twice = jnp.where(col_twice >= grid_cols, col_twice - 2.0 * grid_cols, col_twice)
        col_twice = jnp.where(col_twice < -grid_cols, col_twice + 2.0 * grid_cols, col_twice)
        col_gap = 0.5 * col_twice
        distance = row_gap * row_gap + col_gap * col_gap
        tapering = jnp.exp(-distance / (2.0 * LOC_RADIUS * LOC_RADIUS))
        weight = tapering / (sig * sig)
        rhs = jnp.where(lane <= members, blk, 0.0) * weight
        out_ref[t] = lax.dot_general(
            blk[:, :members],
            rhs,
            (((0,), (0,)), ((), ())),
            precision=highest,
            preferred_element_type=jnp.float32,
        )


def gram_and_forcing(window, aux, picks, row_first, tile_cols, grid_cols):
    tile_count = picks.shape[0]
    tb = 8 if tile_count % 8 == 0 else 1
    members, window_len = window.shape
    width = -(-(members + 8) // 128) * 128
    kernel = functools.partial(
        gram_kernel, tb=tb, tile_cols=tile_cols, grid_cols=grid_cols, members=members
    )
    meta = jnp.reshape(row_first, (1,)).astype(jnp.int32)
    return pl.pallas_call(
        kernel,
        grid_spec=pltpu.PrefetchScalarGridSpec(
            num_scalar_prefetch=2,
            grid=(tile_count // tb,),
            in_specs=[
                pl.BlockSpec((members, window_len), lambda s, p, m: (0, 0)),
                pl.BlockSpec(aux.shape, lambda s, p, m: (0, 0)),
            ],
            out_specs=pl.BlockSpec((tb, members, width), lambda s, p, m: (s, 0, 0)),
            scratch_shapes=[
                pltpu.VMEM((window_len, width), jnp.float32),
                pltpu.VMEM((tb * OBS_TILE, width), jnp.float32),
            ],
        ),
        out_shape=jax.ShapeDtypeStruct((tile_count, members, width), jnp.float32),
        compiler_params=pltpu.CompilerParams(dimension_semantics=("arbitrary",)),
    )(picks.reshape(-1), meta, window, aux)


def analyze(ensemble_block, window, aux, picks, row_first, grid_cols):
    members, block_rows, block_cols = ensemble_block.shape
    tile_cols = block_cols // TILE_COLS
    tile_count = block_rows * tile_cols
    moments = gram_and_forcing(
        window, aux, picks.reshape(tile_count, -1), row_first, tile_cols, grid_cols
    )
    gram_matrix = moments[:, :, :members]
    forcing = moments[:, :, members]
    identity = jnp.eye(members, dtype=jnp.float32)
    system = gram_matrix + (members - 1.0) * identity
    frob_norm = jnp.sqrt(jnp.sum(system * system, axis=(1, 2)))
    iterate = system / frob_norm[:, None, None]
    factor = 1.5 * identity - 0.5 * iterate
    iterate = jnp.einsum("nij,njk->nik", iterate, factor, precision=highest)
    inverse_root = factor
    for sweep_index in range(1, NS_ITERS):
        factor = 1.5 * identity - 0.5 * jnp.einsum(
            "nij,njk->nik", inverse_root, iterate, precision=highest
        )
        iterate = jnp.einsum("nij,njk->nik", iterate, factor, precision=highest)
        inverse_root = jnp.einsum("nij,njk->nik", factor, inverse_root, precision=highest)
    half_step = jnp.einsum("nkj,nj->nk", inverse_root, forcing, precision=highest)
    mean_weight = (
        jnp.einsum("nkj,nj->nk", inverse_root, half_step, precision=highest) / frob_norm[:, None]
    )
    transform = (
        jnp.sqrt(members - 1.0) * inverse_root / jnp.sqrt(frob_norm)[:, None, None]
        + mean_weight[:, :, None]
    )
    tile_cells = ensemble_block.reshape(members, tile_count, TILE_COLS)
    centre_mean = jnp.mean(tile_cells, axis=0)
    spread = tile_cells - centre_mean
    analysis = centre_mean + jnp.einsum("jnt,njk->knt", spread, transform, precision=highest)
    return analysis.reshape(members, block_rows, block_cols)


def on_device(
    ensemble,
    spreading_number,
    zonal_transport_ratio,
    meridional_transport_ratio,
    ocean_mask,
    obs_loc,
    obs_value,
    obs_sigma,
    tile_obs,
):
    mem_dev, row_count, col_count = ensemble.shape
    liquid_cell_flags = ocean_mask.astype(jnp.float32)
    level_state_grid = liquid_cell_flags * ensemble
    for prior_step_tally in range(2):
        haloed_state_grid = padded(level_state_grid, (("space", 1),), 1)
        level_state_grid = propagate_prior_state(
            haloed_state_grid,
            spreading_number,
            zonal_transport_ratio,
            meridional_transport_ratio,
            liquid_cell_flags,
        )
    space_index = lax.axis_index("space")
    member_index = lax.axis_index("member")
    obs_dev = obs_loc.shape[0] // lax.axis_size("space")
    flattened = level_state_grid.reshape(mem_dev, row_count * col_count)
    own_loc = lax.dynamic_slice_in_dim(obs_loc, space_index * obs_dev, obs_dev) - space_index * (
        row_count * col_count
    )
    own_obs = jnp.take(flattened, own_loc, axis=1)
    rimmed = padded(own_obs, (("space", 1),), obs_dev)
    window = lax.all_gather(rimmed, "member", axis=0, tiled=True)
    window_len = window.shape[1]

    def window_of(values, fill):
        rim = jnp.full((obs_dev,), fill, values.dtype)
        return lax.dynamic_slice_in_dim(
            jnp.concatenate([rim, values, rim]), space_index * obs_dev, window_len
        )

    window_loc = window_of(obs_loc, 0)
    aux = jnp.concatenate(
        [
            window_of(obs_value, 0.0)[None],
            window_of(obs_sigma, 1.0)[None],
            (window_loc // col_count).astype(jnp.float32)[None],
            (window_loc % col_count).astype(jnp.float32)[None],
            jnp.zeros((4, window_len), jnp.float32),
        ],
        axis=0,
    )
    first_obs = (space_index - 1) * obs_dev
    cell_block = lax.all_to_all(level_state_grid, "member", split_axis=1, concat_axis=0, tiled=True)
    block_rows = cell_block.shape[1]
    tile_picks = lax.dynamic_slice_in_dim(tile_obs, member_index * block_rows, block_rows, 0)
    local_picks = jnp.clip(tile_picks - first_obs, 0, window_len - 1)
    row_first = space_index * row_count + member_index * block_rows
    updated = analyze(cell_block, window, aux, local_picks, row_first, col_count)
    result = lax.all_to_all(updated, "member", split_axis=0, concat_axis=1, tiled=True)
    return result


def solution(mesh):
    in_specs = (
        P("member", "space", None),
        P("space", None),
        P("space", None),
        P("space", None),
        P("space", None),
        P(),
        P(),
        P(),
        P("space", None, None),
    )
    out_specs = P("member", "space", None)
    return jax.shard_map(
        on_device, mesh=mesh, in_specs=in_specs, out_specs=out_specs, check_vma=False
    )
```

```python
import functools
import jax
import jax.numpy as jnp
from jax import lax
from jax.experimental import pallas as pl
from jax.experimental.pallas import tpu as pltpu
from jax.sharding import PartitionSpec as P


TILE_COLS = 128
OBS_TILE = 256
LOC_RADIUS = 96
NS_ITERS = 6


highest = lax.Precision.HIGHEST


def padded(cells, sides, width):
    for axis, dim in sides:
        count = lax.axis_size(axis)
        ends = count - 1
        head = lax.slice_in_dim(cells, 0, width, axis=dim)
        tail = lax.slice_in_dim(cells, cells.shape[dim] - width, cells.shape[dim], axis=dim)
        cells = jnp.concatenate(
            [
                lax.ppermute(tail, axis, [(i, (i + 1) % count) for i in range(ends)]),
                cells,
                lax.ppermute(head, axis, [((i + 1) % count, i) for i in range(ends)]),
            ],
            axis=dim,
        )
    return cells


def exchange(blocks, axis, place_dim, place_len):
    count = lax.axis_size(axis)
    me = lax.axis_index(axis)
    shape = list(blocks.shape[1:])
    shape[place_dim] *= count
    result = jnp.zeros(shape, blocks.dtype)
    result = lax.dynamic_update_slice_in_dim(
        result, lax.dynamic_index_in_dim(blocks, me, keepdims=False), me * place_len, place_dim
    )
    for shift in range(1, count):
        partner = jnp.bitwise_xor(me, shift)
        sent = lax.dynamic_index_in_dim(blocks, partner, keepdims=False)
        got = lax.ppermute(sent, axis, [(i, i ^ shift) for i in range(count)])
        result = lax.dynamic_update_slice_in_dim(result, got, partner * place_len, place_dim)
    return result


def propagate_prior_state(
    haloed_state_grid,
    spreading_number,
    zonal_transport_ratio,
    meridional_transport_ratio,
    liquid_cell_flags,
):
    centre = haloed_state_grid[:, 1:-1, :]
    northern = haloed_state_grid[:, 2:, :]
    southern = haloed_state_grid[:, :-2, :]
    eastern = jnp.roll(centre, -1, axis=2)
    western = jnp.roll(centre, 1, axis=2)
    laplace = northern + southern + eastern + western - 4.0 * centre
    advect = (
        zonal_transport_ratio * (eastern - western) * 0.5
        + meridional_transport_ratio * (northern - southern) * 0.5
    )
    return liquid_cell_flags * (centre + spreading_number * laplace - advect)


def gram_kernel(
    picks_ref, meta_ref, window_ref, aux_ref, out_ref, table_ref, buf_ref, *, tb, tile_cols, grid_cols, members
):
    step = pl.program_id(0)
    base = step * (tb * OBS_TILE)
    width = table_ref.shape[1]

    @pl.when(step == 0)
    def _():
        def build(c, carry):
            start = pl.multiple_of(c * 128, 128)
            values = window_ref[:, pl.ds(start, 128)]
            mean = jnp.mean(values, axis=0, keepdims=True)
            extra = aux_ref[:, pl.ds(start, 128)]
            first = lax.broadcasted_iota(jnp.int32, extra.shape, 0) == 0
            extra = jnp.where(first, extra - mean, extra)
            rows = jnp.concatenate(
                [values - mean, extra, jnp.zeros((width - members - 8, 128), jnp.float32)], axis=0
            )
            table_ref[pl.ds(start, 128), :] = rows.T
            return carry

        lax.fori_loop(0, table_ref.shape[0] // 128, build, 0)


    def gather(j, carry):
        for u in range(8):
            i = j * 8 + u
            idx = picks_ref[base + i]
            buf_ref[pl.ds(i, 1), :] = table_ref[pl.ds(idx, 1), :]
        return carry

    lax.fori_loop(0, tb * OBS_TILE // 8, gather, 0)
    row_first = meta_ref[0]
    lane = lax.broadcasted_iota(jnp.int32, (OBS_TILE, width), 1)
    for t in range(tb):
        n = step * tb + t
        tile_row = jnp.full((OBS_TILE, 1), row_first + n // tile_cols, jnp.int32).astype(jnp.float32)
        tile_start = jnp.full((OBS_TILE, 1), TILE_COLS * (n % tile_cols), jnp.int32).astype(jnp.float32)
        blk = buf_ref[pl.ds(t * OBS_TILE, OBS_TILE), :]
        sig = blk[:, members + 1 : members + 2]
        orow = blk[:, members + 2 : members + 3]
        ocol = blk[:, members + 3 : members + 4]
        row_gap = orow - tile_row
        col_twice = 2.0 * ocol - 2.0 * tile_start - float(TILE_COLS - 1)
        col_twice = jnp.where(col_twice >= grid_cols, col_twice - 2.0 * grid_cols, col_twice)
        col_twice = jnp.where(col_twice < -grid_cols, col_twice + 2.0 * grid_cols, col_twice)
        col_gap = 0.5 * col_twice
        distance = row_gap * row_gap + col_gap * col_gap
        tapering = jnp.exp(-distance / (2.0 * LOC_RADIUS * LOC_RADIUS))
        weight = tapering / (sig * sig)
        rhs = jnp.where(lane <= members, blk, 0.0) * weight
        out_ref[t] = lax.dot_general(
            blk[:, :members],
            rhs,
            (((0,), (0,)), ((), ())),
            precision=highest,
            preferred_element_type=jnp.float32,
        )


def gram_and_forcing(window, aux, picks, row_first, tile_cols, grid_cols):
    tile_count = picks.shape[0]
    tb = 8 if tile_count % 8 == 0 else 1
    members, window_len = window.shape
    width = -(-(members + 8) // 128) * 128
    kernel = functools.partial(
        gram_kernel, tb=tb, tile_cols=tile_cols, grid_cols=grid_cols, members=members
    )
    meta = jnp.reshape(row_first, (1,)).astype(jnp.int32)
    return pl.pallas_call(
        kernel,
        grid_spec=pltpu.PrefetchScalarGridSpec(
            num_scalar_prefetch=2,
            grid=(tile_count // tb,),
            in_specs=[
                pl.BlockSpec((members, window_len), lambda s, p, m: (0, 0)),
                pl.BlockSpec(aux.shape, lambda s, p, m: (0, 0)),
            ],
            out_specs=pl.BlockSpec((tb, members, width), lambda s, p, m: (s, 0, 0)),
            scratch_shapes=[
                pltpu.VMEM((window_len, width), jnp.float32),
                pltpu.VMEM((tb * OBS_TILE, width), jnp.float32),
            ],
        ),
        out_shape=jax.ShapeDtypeStruct((tile_count, members, width), jnp.float32),
        compiler_params=pltpu.CompilerParams(dimension_semantics=("arbitrary",)),
    )(picks.reshape(-1), meta, window, aux)


def analyze(ensemble_block, window, aux, picks, row_first, grid_cols):
    members, block_rows, block_cols = ensemble_block.shape
    tile_cols = block_cols // TILE_COLS
    tile_count = block_rows * tile_cols
    moments = gram_and_forcing(
        window, aux, picks.reshape(tile_count, -1), row_first, tile_cols, grid_cols
    )
    gram_matrix = moments[:, :, :members]
    forcing = moments[:, :, members]
    identity = jnp.eye(members, dtype=jnp.float32)
    system = gram_matrix + (members - 1.0) * identity
    frob_norm = jnp.sqrt(jnp.sum(system * system, axis=(1, 2)))
    iterate = system / frob_norm[:, None, None]
    factor = 1.5 * identity - 0.5 * iterate
    iterate = jnp.einsum("nij,njk->nik", iterate, factor, precision=highest)
    inverse_root = factor
    for _ in range(1, NS_ITERS):
        factor = 1.5 * identity - 0.5 * jnp.einsum(
            "nij,njk->nik", inverse_root, iterate, precision=highest
        )
        iterate = jnp.einsum("nij,njk->nik", iterate, factor, precision=highest)
        inverse_root = jnp.einsum("nij,njk->nik", factor, inverse_root, precision=highest)
    half_step = jnp.einsum("nkj,nj->nk", inverse_root, forcing, precision=highest)
    mean_weight = (
        jnp.einsum("nkj,nj->nk", inverse_root, half_step, precision=highest) / frob_norm[:, None]
    )
    transform = (
        jnp.sqrt(members - 1.0) * inverse_root / jnp.sqrt(frob_norm)[:, None, None]
        + mean_weight[:, :, None]
    )
    tile_cells = ensemble_block.reshape(members, tile_count, TILE_COLS)
    centre_mean = jnp.mean(tile_cells, axis=0)
    spread = tile_cells - centre_mean
    analysis = centre_mean + jnp.einsum("jnt,njk->knt", spread, transform, precision=highest)
    return analysis.reshape(members, block_rows, block_cols)


def on_device(
    ensemble,
    spreading_number,
    zonal_transport_ratio,
    meridional_transport_ratio,
    ocean_mask,
    obs_loc,
    obs_value,
    obs_sigma,
    tile_obs,
):
    mem_dev, row_count, col_count = ensemble.shape
    liquid_cell_flags = ocean_mask.astype(jnp.float32)
    level_state_grid = liquid_cell_flags * ensemble
    for _ in range(2):
        haloed_state_grid = padded(level_state_grid, (("space", 1),), 1)
        level_state_grid = propagate_prior_state(
            haloed_state_grid,
            spreading_number,
            zonal_transport_ratio,
            meridional_transport_ratio,
            liquid_cell_flags,
        )
    space_index = lax.axis_index("space")
    member_index = lax.axis_index("member")
    obs_dev = obs_loc.shape[0] // lax.axis_size("space")
    flattened = level_state_grid.reshape(mem_dev, row_count * col_count)
    own_loc = lax.dynamic_slice_in_dim(obs_loc, space_index * obs_dev, obs_dev) - space_index * (
        row_count * col_count
    )
    own_obs = jnp.take(flattened, own_loc, axis=1)
    rimmed = padded(own_obs, (("space", 1),), obs_dev)
    window = lax.all_gather(rimmed, "member", axis=0, tiled=True)
    window_len = window.shape[1]

    def window_of(values, fill):
        rim = jnp.full((obs_dev,), fill, values.dtype)
        return lax.dynamic_slice_in_dim(
            jnp.concatenate([rim, values, rim]), space_index * obs_dev, window_len
        )

    window_loc = window_of(obs_loc, 0)
    aux = jnp.concatenate(
        [
            window_of(obs_value, 0.0)[None],
            window_of(obs_sigma, 1.0)[None],
            (window_loc // col_count).astype(jnp.float32)[None],
            (window_loc % col_count).astype(jnp.float32)[None],
            jnp.zeros((4, window_len), jnp.float32),
        ],
        axis=0,
    )
    first_obs = (space_index - 1) * obs_dev
    member_count = lax.axis_size("member")
    block_rows = row_count // member_count
    cell_block = exchange(
        level_state_grid.reshape(mem_dev, member_count, block_rows, col_count).transpose(
            1, 0, 2, 3
        ),
        "member",
        0,
        mem_dev,
    )
    tile_picks = lax.dynamic_slice_in_dim(tile_obs, member_index * block_rows, block_rows, 0)
    local_picks = jnp.clip(tile_picks - first_obs, 0, window_len - 1)
    row_first = space_index * row_count + member_index * block_rows
    updated = analyze(cell_block, window, aux, local_picks, row_first, col_count)
    result = exchange(
        updated.reshape(member_count, mem_dev, block_rows, col_count), "member", 1, block_rows
    )
    return result


def solution(mesh):
    in_specs = (
        P("member", "space", None),
        P("space", None),
        P("space", None),
        P("space", None),
        P("space", None),
        P(),
        P(),
        P(),
        P("space", None, None),
    )
    out_specs = P("member", "space", None)

    return jax.shard_map(on_device, mesh=mesh, in_specs=in_specs, out_specs=out_specs, check_vma=False)
```

```python
import functools
import jax
import jax.numpy as jnp
from jax import lax
from jax.experimental import pallas as pl
from jax.experimental.pallas import tpu as pltpu
from jax.sharding import PartitionSpec as P


TILE_COLS = 128
OBS_TILE = 256
LOC_RADIUS = 96
NS_ITERS = 6


highest = lax.Precision.HIGHEST


def padded(cells, sides, width):
    for axis, dim in sides:
        count = lax.axis_size(axis)
        ends = count - 1
        head = lax.slice_in_dim(cells, 0, width, axis=dim)
        tail = lax.slice_in_dim(cells, cells.shape[dim] - width, cells.shape[dim], axis=dim)
        cells = jnp.concatenate(
            [
                lax.ppermute(tail, axis, [(i, (i + 1) % count) for i in range(ends)]),
                cells,
                lax.ppermute(head, axis, [((i + 1) % count, i) for i in range(ends)]),
            ],
            axis=dim,
        )
    return cells


def exchange(blocks, axis, place_dim, place_len):
    count = lax.axis_size(axis)
    me = lax.axis_index(axis)
    shape = list(blocks.shape[1:])
    shape[place_dim] *= count
    result = jnp.zeros(shape, blocks.dtype)
    result = lax.dynamic_update_slice_in_dim(
        result, lax.dynamic_index_in_dim(blocks, me, keepdims=False), me * place_len, place_dim
    )
    for shift in range(1, count):
        partner = jnp.bitwise_xor(me, shift)
        sent = lax.dynamic_index_in_dim(blocks, partner, keepdims=False)
        got = lax.ppermute(sent, axis, [(i, i ^ shift) for i in range(count)])
        result = lax.dynamic_update_slice_in_dim(result, got, partner * place_len, place_dim)
    return result


def gather_members(block, axis):
    count = lax.axis_size(axis)
    me = lax.axis_index(axis)
    rows = block.shape[0]
    result = jnp.zeros((count * rows,) + block.shape[1:], block.dtype)
    result = lax.dynamic_update_slice_in_dim(result, block, me * rows, 0)
    for shift in range(1, count):
        partner = jnp.bitwise_xor(me, shift)
        got = lax.ppermute(block, axis, [(i, i ^ shift) for i in range(count)])
        result = lax.dynamic_update_slice_in_dim(result, got, partner * rows, 0)
    return result


def propagate_prior_state(
    haloed_state_grid,
    spreading_number,
    zonal_transport_ratio,
    meridional_transport_ratio,
    liquid_cell_flags,
):
    centre = haloed_state_grid[:, 1:-1, :]
    northern = haloed_state_grid[:, 2:, :]
    southern = haloed_state_grid[:, :-2, :]
    eastern = jnp.roll(centre, -1, axis=2)
    western = jnp.roll(centre, 1, axis=2)
    laplace = northern + southern + eastern + western - 4.0 * centre
    advect = (
        zonal_transport_ratio * (eastern - western) * 0.5
        + meridional_transport_ratio * (northern - southern) * 0.5
    )
    return liquid_cell_flags * (centre + spreading_number * laplace - advect)


def gram_kernel(
    picks_ref, meta_ref, window_ref, aux_ref, out_ref, table_ref, buf_ref, *, tb, tile_cols, grid_cols, members
):
    step = pl.program_id(0)
    base = step * (tb * OBS_TILE)
    width = table_ref.shape[1]

    @pl.when(step == 0)
    def _():
        def build(c, carry):
            start = pl.multiple_of(c * 128, 128)
            values = window_ref[:, pl.ds(start, 128)]
            mean = jnp.mean(values, axis=0, keepdims=True)
            extra = aux_ref[:, pl.ds(start, 128)]
            first = lax.broadcasted_iota(jnp.int32, extra.shape, 0) == 0
            extra = jnp.where(first, extra - mean, extra)
            rows = jnp.concatenate(
                [values - mean, extra, jnp.zeros((width - members - 8, 128), jnp.float32)], axis=0
            )
            table_ref[pl.ds(start, 128), :] = rows.T
            return carry

        lax.fori_loop(0, table_ref.shape[0] // 128, build, 0)


    def gather(j, carry):
        for u in range(8):
            i = j * 8 + u
            idx = picks_ref[base + i]
            buf_ref[pl.ds(i, 1), :] = table_ref[pl.ds(idx, 1), :]
        return carry

    lax.fori_loop(0, tb * OBS_TILE // 8, gather, 0)
    row_first = meta_ref[0]
    lane = lax.broadcasted_iota(jnp.int32, (OBS_TILE, width), 1)
    for t in range(tb):
        n = step * tb + t
        tile_row = jnp.full((OBS_TILE, 1), row_first + n // tile_cols, jnp.int32).astype(jnp.float32)
        tile_start = jnp.full((OBS_TILE, 1), TILE_COLS * (n % tile_cols), jnp.int32).astype(jnp.float32)
        blk = buf_ref[pl.ds(t * OBS_TILE, OBS_TILE), :]
        sig = blk[:, members + 1 : members + 2]
        orow = blk[:, members + 2 : members + 3]
        ocol = blk[:, members + 3 : members + 4]
        row_gap = orow - tile_row
        col_twice = 2.0 * ocol - 2.0 * tile_start - float(TILE_COLS - 1)
        col_twice = jnp.where(col_twice >= grid_cols, col_twice - 2.0 * grid_cols, col_twice)
        col_twice = jnp.where(col_twice < -grid_cols, col_twice + 2.0 * grid_cols, col_twice)
        col_gap = 0.5 * col_twice
        distance = row_gap * row_gap + col_gap * col_gap
        tapering = jnp.exp(-distance / (2.0 * LOC_RADIUS * LOC_RADIUS))
        weight = tapering / (sig * sig)
        rhs = jnp.where(lane <= members, blk, 0.0) * weight
        out_ref[t] = lax.dot_general(
            blk[:, :members],
            rhs,
            (((0,), (0,)), ((), ())),
            precision=highest,
            preferred_element_type=jnp.float32,
        )


def gram_and_forcing(window, aux, picks, row_first, tile_cols, grid_cols):
    tile_count = picks.shape[0]
    tb = 8 if tile_count % 8 == 0 else 1
    members, window_len = window.shape
    width = -(-(members + 8) // 128) * 128
    kernel = functools.partial(
        gram_kernel, tb=tb, tile_cols=tile_cols, grid_cols=grid_cols, members=members
    )
    meta = jnp.reshape(row_first, (1,)).astype(jnp.int32)
    return pl.pallas_call(
        kernel,
        grid_spec=pltpu.PrefetchScalarGridSpec(
            num_scalar_prefetch=2,
            grid=(tile_count // tb,),
            in_specs=[
                pl.BlockSpec((members, window_len), lambda s, p, m: (0, 0)),
                pl.BlockSpec(aux.shape, lambda s, p, m: (0, 0)),
            ],
            out_specs=pl.BlockSpec((tb, members, width), lambda s, p, m: (s, 0, 0)),
            scratch_shapes=[
                pltpu.VMEM((window_len, width), jnp.float32),
                pltpu.VMEM((tb * OBS_TILE, width), jnp.float32),
            ],
        ),
        out_shape=jax.ShapeDtypeStruct((tile_count, members, width), jnp.float32),
        compiler_params=pltpu.CompilerParams(dimension_semantics=("arbitrary",)),
    )(picks.reshape(-1), meta, window, aux)


def analyze(ensemble_block, window, aux, picks, row_first, grid_cols):
    members, block_rows, block_cols = ensemble_block.shape
    tile_cols = block_cols // TILE_COLS
    tile_count = block_rows * tile_cols
    moments = gram_and_forcing(
        window, aux, picks.reshape(tile_count, -1), row_first, tile_cols, grid_cols
    )
    gram_matrix = moments[:, :, :members]
    forcing = moments[:, :, members]
    identity = jnp.eye(members, dtype=jnp.float32)
    system = gram_matrix + (members - 1.0) * identity
    frob_norm = jnp.sqrt(jnp.sum(system * system, axis=(1, 2)))
    iterate = system / frob_norm[:, None, None]
    factor = 1.5 * identity - 0.5 * iterate
    iterate = jnp.einsum("nij,njk->nik", iterate, factor, precision=highest)
    inverse_root = factor
    for _ in range(1, NS_ITERS):
        factor = 1.5 * identity - 0.5 * jnp.einsum(
            "nij,njk->nik", inverse_root, iterate, precision=highest
        )
        iterate = jnp.einsum("nij,njk->nik", iterate, factor, precision=highest)
        inverse_root = jnp.einsum("nij,njk->nik", factor, inverse_root, precision=highest)
    half_step = jnp.einsum("nkj,nj->nk", inverse_root, forcing, precision=highest)
    mean_weight = (
        jnp.einsum("nkj,nj->nk", inverse_root, half_step, precision=highest) / frob_norm[:, None]
    )
    transform = (
        jnp.sqrt(members - 1.0) * inverse_root / jnp.sqrt(frob_norm)[:, None, None]
        + mean_weight[:, :, None]
    )
    tile_cells = ensemble_block.reshape(members, tile_count, TILE_COLS)
    centre_mean = jnp.mean(tile_cells, axis=0)
    spread = tile_cells - centre_mean
    analysis = centre_mean + jnp.einsum("jnt,njk->knt", spread, transform, precision=highest)
    return analysis.reshape(members, block_rows, block_cols)


def on_device(
    ensemble,
    spreading_number,
    zonal_transport_ratio,
    meridional_transport_ratio,
    ocean_mask,
    obs_loc,
    obs_value,
    obs_sigma,
    tile_obs,
):
    mem_dev, row_count, col_count = ensemble.shape
    liquid_cell_flags = ocean_mask.astype(jnp.float32)
    level_state_grid = liquid_cell_flags * ensemble
    for _ in range(2):
        haloed_state_grid = padded(level_state_grid, (("space", 1),), 1)
        level_state_grid = propagate_prior_state(
            haloed_state_grid,
            spreading_number,
            zonal_transport_ratio,
            meridional_transport_ratio,
            liquid_cell_flags,
        )
    space_index = lax.axis_index("space")
    member_index = lax.axis_index("member")
    obs_dev = obs_loc.shape[0] // lax.axis_size("space")
    flattened = level_state_grid.reshape(mem_dev, row_count * col_count)
    own_loc = lax.dynamic_slice_in_dim(obs_loc, space_index * obs_dev, obs_dev) - space_index * (
        row_count * col_count
    )
    own_obs = jnp.take(flattened, own_loc, axis=1)
    rimmed = padded(own_obs, (("space", 1),), obs_dev)
    window = gather_members(rimmed, "member")
    window_len = window.shape[1]

    def window_of(values, fill):
        rim = jnp.full((obs_dev,), fill, values.dtype)
        return lax.dynamic_slice_in_dim(
            jnp.concatenate([rim, values, rim]), space_index * obs_dev, window_len
        )

    window_loc = window_of(obs_loc, 0)
    aux = jnp.concatenate(
        [
            window_of(obs_value, 0.0)[None],
            window_of(obs_sigma, 1.0)[None],
            (window_loc // col_count).astype(jnp.float32)[None],
            (window_loc % col_count).astype(jnp.float32)[None],
            jnp.zeros((4, window_len), jnp.float32),
        ],
        axis=0,
    )
    first_obs = (space_index - 1) * obs_dev
    member_count = lax.axis_size("member")
    block_rows = row_count // member_count
    cell_block = exchange(
        level_state_grid.reshape(mem_dev, member_count, block_rows, col_count).transpose(
            1, 0, 2, 3
        ),
        "member",
        0,
        mem_dev,
    )
    tile_picks = lax.dynamic_slice_in_dim(tile_obs, member_index * block_rows, block_rows, 0)
    local_picks = jnp.clip(tile_picks - first_obs, 0, window_len - 1)
    row_first = space_index * row_count + member_index * block_rows
    updated = analyze(cell_block, window, aux, local_picks, row_first, col_count)
    result = exchange(
        updated.reshape(member_count, mem_dev, block_rows, col_count), "member", 1, block_rows
    )
    return result


def solution(mesh):
    in_specs = (
        P("member", "space", None),
        P("space", None),
        P("space", None),
        P("space", None),
        P("space", None),
        P(),
        P(),
        P(),
        P("space", None, None),
    )
    out_specs = P("member", "space", None)

    return jax.shard_map(on_device, mesh=mesh, in_specs=in_specs, out_specs=out_specs, check_vma=False)
```

```python
import functools
import jax
import jax.numpy as jnp
from jax import lax
from jax.experimental import pallas as pl
from jax.experimental.pallas import tpu as pltpu
from jax.sharding import PartitionSpec as P


TILE_COLS = 128
OBS_TILE = 256
LOC_RADIUS = 96
NS_ITERS = 6


highest = lax.Precision.HIGHEST


def padded(cells, sides, width):
    for axis, dim in sides:
        count = lax.axis_size(axis)
        ends = count - 1
        head = lax.slice_in_dim(cells, 0, width, axis=dim)
        tail = lax.slice_in_dim(cells, cells.shape[dim] - width, cells.shape[dim], axis=dim)
        cells = jnp.concatenate(
            [
                lax.ppermute(tail, axis, [(i, (i + 1) % count) for i in range(ends)]),
                cells,
                lax.ppermute(head, axis, [((i + 1) % count, i) for i in range(ends)]),
            ],
            axis=dim,
        )
    return cells


def exchange(blocks, axis, place_dim, place_len):
    count = lax.axis_size(axis)
    me = lax.axis_index(axis)
    shape = list(blocks.shape[1:])
    shape[place_dim] *= count
    result = jnp.zeros(shape, blocks.dtype)
    result = lax.dynamic_update_slice_in_dim(
        result, lax.dynamic_index_in_dim(blocks, me, keepdims=False), me * place_len, place_dim
    )
    for shift in range(1, count):
        partner = jnp.bitwise_xor(me, shift)
        sent = lax.dynamic_index_in_dim(blocks, partner, keepdims=False)
        got = lax.ppermute(sent, axis, [(i, i ^ shift) for i in range(count)])
        result = lax.dynamic_update_slice_in_dim(result, got, partner * place_len, place_dim)
    return result


def gather_members(block, axis):
    count = lax.axis_size(axis)
    me = lax.axis_index(axis)
    rows = block.shape[0]
    result = jnp.zeros((count * rows,) + block.shape[1:], block.dtype)
    result = lax.dynamic_update_slice_in_dim(result, block, me * rows, 0)
    for shift in range(1, count):
        partner = jnp.bitwise_xor(me, shift)
        got = lax.ppermute(block, axis, [(i, i ^ shift) for i in range(count)])
        result = lax.dynamic_update_slice_in_dim(result, got, partner * rows, 0)
    return result


def propagate_prior_state(
    haloed_state_grid,
    spreading_number,
    zonal_transport_ratio,
    meridional_transport_ratio,
    liquid_cell_flags,
):
    centre = haloed_state_grid[:, 1:-1, :]
    northern = haloed_state_grid[:, 2:, :]
    southern = haloed_state_grid[:, :-2, :]
    eastern = jnp.roll(centre, -1, axis=2)
    western = jnp.roll(centre, 1, axis=2)
    laplace = northern + southern + eastern + western - 4.0 * centre
    advect = (
        zonal_transport_ratio * (eastern - western) * 0.5
        + meridional_transport_ratio * (northern - southern) * 0.5
    )
    return liquid_cell_flags * (centre + spreading_number * laplace - advect)


def gram_kernel(
    picks_ref, meta_ref, window_ref, aux_ref, out_ref, table_ref, buf_ref, *, tb, tile_cols, grid_cols, members
):
    step = pl.program_id(0)
    base = step * (tb * OBS_TILE)
    width = table_ref.shape[1]

    @pl.when(step == 0)
    def _():
        def build(c, carry):
            start = pl.multiple_of(c * 128, 128)
            values = window_ref[:, pl.ds(start, 128)]
            mean = jnp.mean(values, axis=0, keepdims=True)
            extra = aux_ref[:, pl.ds(start, 128)]
            first = lax.broadcasted_iota(jnp.int32, extra.shape, 0) == 0
            extra = jnp.where(first, extra - mean, extra)
            rows = jnp.concatenate(
                [values - mean, extra, jnp.zeros((width - members - 8, 128), jnp.float32)], axis=0
            )
            table_ref[pl.ds(start, 128), :] = rows.T
            return carry

        lax.fori_loop(0, table_ref.shape[0] // 128, build, 0)


    unroll = 32

    def gather(j, carry):
        first = pl.multiple_of(j * unroll, unroll)
        at = base + first
        for u in range(unroll):
            idx = picks_ref[at + u]
            buf_ref[pl.ds(first + u, 1), :] = table_ref[pl.ds(idx, 1), :]
        return carry

    lax.fori_loop(0, tb * OBS_TILE // unroll, gather, 0)
    row_first = meta_ref[0]
    lane = lax.broadcasted_iota(jnp.int32, (OBS_TILE, width), 1)
    for t in range(tb):
        n = step * tb + t
        tile_row = jnp.full((OBS_TILE, 1), row_first + n // tile_cols, jnp.int32).astype(jnp.float32)
        tile_start = jnp.full((OBS_TILE, 1), TILE_COLS * (n % tile_cols), jnp.int32).astype(jnp.float32)
        blk = buf_ref[pl.ds(t * OBS_TILE, OBS_TILE), :]
        sig = blk[:, members + 1 : members + 2]
        orow = blk[:, members + 2 : members + 3]
        ocol = blk[:, members + 3 : members + 4]
        row_gap = orow - tile_row
        col_twice = 2.0 * ocol - 2.0 * tile_start - float(TILE_COLS - 1)
        col_twice = jnp.where(col_twice >= grid_cols, col_twice - 2.0 * grid_cols, col_twice)
        col_twice = jnp.where(col_twice < -grid_cols, col_twice + 2.0 * grid_cols, col_twice)
        col_gap = 0.5 * col_twice
        distance = row_gap * row_gap + col_gap * col_gap
        tapering = jnp.exp(-distance / (2.0 * LOC_RADIUS * LOC_RADIUS))
        weight = tapering / (sig * sig)
        rhs = jnp.where(lane <= members, blk, 0.0) * weight
        out_ref[t] = lax.dot_general(
            blk[:, :members],
            rhs,
            (((0,), (0,)), ((), ())),
            precision=highest,
            preferred_element_type=jnp.float32,
        )


def gram_and_forcing(window, aux, picks, row_first, tile_cols, grid_cols):
    tile_count = picks.shape[0]
    tb = 8 if tile_count % 8 == 0 else 1
    members, window_len = window.shape
    width = -(-(members + 8) // 128) * 128
    kernel = functools.partial(
        gram_kernel, tb=tb, tile_cols=tile_cols, grid_cols=grid_cols, members=members
    )
    meta = jnp.reshape(row_first, (1,)).astype(jnp.int32)
    return pl.pallas_call(
        kernel,
        grid_spec=pltpu.PrefetchScalarGridSpec(
            num_scalar_prefetch=2,
            grid=(tile_count // tb,),
            in_specs=[
                pl.BlockSpec((members, window_len), lambda s, p, m: (0, 0)),
                pl.BlockSpec(aux.shape, lambda s, p, m: (0, 0)),
            ],
            out_specs=pl.BlockSpec((tb, members, width), lambda s, p, m: (s, 0, 0)),
            scratch_shapes=[
                pltpu.VMEM((window_len, width), jnp.float32),
                pltpu.VMEM((tb * OBS_TILE, width), jnp.float32),
            ],
        ),
        out_shape=jax.ShapeDtypeStruct((tile_count, members, width), jnp.float32),
        compiler_params=pltpu.CompilerParams(dimension_semantics=("arbitrary",)),
    )(picks.reshape(-1), meta, window, aux)


def analyze(ensemble_block, window, aux, picks, row_first, grid_cols):
    members, block_rows, block_cols = ensemble_block.shape
    tile_cols = block_cols // TILE_COLS
    tile_count = block_rows * tile_cols
    moments = gram_and_forcing(
        window, aux, picks.reshape(tile_count, -1), row_first, tile_cols, grid_cols
    )
    gram_matrix = moments[:, :, :members]
    forcing = moments[:, :, members]
    identity = jnp.eye(members, dtype=jnp.float32)
    system = gram_matrix + (members - 1.0) * identity
    frob_norm = jnp.sqrt(jnp.sum(system * system, axis=(1, 2)))
    iterate = system / frob_norm[:, None, None]
    factor = 1.5 * identity - 0.5 * iterate
    iterate = jnp.einsum("nij,njk->nik", iterate, factor, precision=lax.Precision.HIGH)
    inverse_root = factor
    for _ in range(1, NS_ITERS):
        factor = 1.5 * identity - 0.5 * jnp.einsum(
            "nij,njk->nik", inverse_root, iterate, precision=lax.Precision.HIGH
        )
        iterate = jnp.einsum("nij,njk->nik", iterate, factor, precision=lax.Precision.HIGH)
        inverse_root = jnp.einsum("nij,njk->nik", factor, inverse_root, precision=lax.Precision.HIGH)
    half_step = jnp.einsum("nkj,nj->nk", inverse_root, forcing, precision=highest)
    mean_weight = (
        jnp.einsum("nkj,nj->nk", inverse_root, half_step, precision=highest) / frob_norm[:, None]
    )
    transform = (
        jnp.sqrt(members - 1.0) * inverse_root / jnp.sqrt(frob_norm)[:, None, None]
        + mean_weight[:, :, None]
    )
    tile_cells = ensemble_block.reshape(members, tile_count, TILE_COLS)
    centre_mean = jnp.mean(tile_cells, axis=0)
    spread = tile_cells - centre_mean
    analysis = centre_mean + jnp.einsum("jnt,njk->knt", spread, transform, precision=highest)
    return analysis.reshape(members, block_rows, block_cols)


def on_device(
    ensemble,
    spreading_number,
    zonal_transport_ratio,
    meridional_transport_ratio,
    ocean_mask,
    obs_loc,
    obs_value,
    obs_sigma,
    tile_obs,
):
    mem_dev, row_count, col_count = ensemble.shape
    liquid_cell_flags = ocean_mask.astype(jnp.float32)
    level_state_grid = liquid_cell_flags * ensemble
    for _ in range(2):
        haloed_state_grid = padded(level_state_grid, (("space", 1),), 1)
        level_state_grid = propagate_prior_state(
            haloed_state_grid,
            spreading_number,
            zonal_transport_ratio,
            meridional_transport_ratio,
            liquid_cell_flags,
        )
    space_index = lax.axis_index("space")
    member_index = lax.axis_index("member")
    obs_dev = obs_loc.shape[0] // lax.axis_size("space")
    flattened = level_state_grid.reshape(mem_dev, row_count * col_count)
    own_loc = lax.dynamic_slice_in_dim(obs_loc, space_index * obs_dev, obs_dev) - space_index * (
        row_count * col_count
    )
    own_obs = jnp.take(flattened, own_loc, axis=1)
    rimmed = padded(own_obs, (("space", 1),), obs_dev)
    window = gather_members(rimmed, "member")
    window_len = window.shape[1]

    def window_of(values, fill):
        rim = jnp.full((obs_dev,), fill, values.dtype)
        return lax.dynamic_slice_in_dim(
            jnp.concatenate([rim, values, rim]), space_index * obs_dev, window_len
        )

    window_loc = window_of(obs_loc, 0)
    aux = jnp.concatenate(
        [
            window_of(obs_value, 0.0)[None],
            window_of(obs_sigma, 1.0)[None],
            (window_loc // col_count).astype(jnp.float32)[None],
            (window_loc % col_count).astype(jnp.float32)[None],
            jnp.zeros((4, window_len), jnp.float32),
        ],
        axis=0,
    )
    first_obs = (space_index - 1) * obs_dev
    member_count = lax.axis_size("member")
    block_rows = row_count // member_count
    cell_block = exchange(
        level_state_grid.reshape(mem_dev, member_count, block_rows, col_count).transpose(
            1, 0, 2, 3
        ),
        "member",
        0,
        mem_dev,
    )
    tile_picks = lax.dynamic_slice_in_dim(tile_obs, member_index * block_rows, block_rows, 0)
    local_picks = jnp.clip(tile_picks - first_obs, 0, window_len - 1)
    row_first = space_index * row_count + member_index * block_rows
    updated = analyze(cell_block, window, aux, local_picks, row_first, col_count)
    result = exchange(
        updated.reshape(member_count, mem_dev, block_rows, col_count), "member", 1, block_rows
    )
    return result


def solution(mesh):
    in_specs = (
        P("member", "space", None),
        P("space", None),
        P("space", None),
        P("space", None),
        P("space", None),
        P(),
        P(),
        P(),
        P("space", None, None),
    )
    out_specs = P("member", "space", None)

    return jax.shard_map(on_device, mesh=mesh, in_specs=in_specs, out_specs=out_specs, check_vma=False)
```

```python
import functools
import jax
import jax.numpy as jnp
from jax import lax
from jax.experimental import pallas as pl
from jax.experimental.pallas import tpu as pltpu
from jax.sharding import PartitionSpec as P


TILE_COLS = 128
OBS_TILE = 256
LOC_RADIUS = 96
NS_ITERS = 6


highest = lax.Precision.HIGHEST


def padded(cells, sides, width):
    for axis, dim in sides:
        count = lax.axis_size(axis)
        ends = count - 1
        head = lax.slice_in_dim(cells, 0, width, axis=dim)
        tail = lax.slice_in_dim(cells, cells.shape[dim] - width, cells.shape[dim], axis=dim)
        cells = jnp.concatenate(
            [
                lax.ppermute(tail, axis, [(i, (i + 1) % count) for i in range(ends)]),
                cells,
                lax.ppermute(head, axis, [((i + 1) % count, i) for i in range(ends)]),
            ],
            axis=dim,
        )
    return cells


def exchange(blocks, axis, place_dim, place_len):
    count = lax.axis_size(axis)
    me = lax.axis_index(axis)
    shape = list(blocks.shape[1:])
    shape[place_dim] *= count
    result = jnp.zeros(shape, blocks.dtype)
    result = lax.dynamic_update_slice_in_dim(
        result, lax.dynamic_index_in_dim(blocks, me, keepdims=False), me * place_len, place_dim
    )
    for shift in range(1, count):
        partner = jnp.bitwise_xor(me, shift)
        sent = lax.dynamic_index_in_dim(blocks, partner, keepdims=False)
        got = lax.ppermute(sent, axis, [(i, i ^ shift) for i in range(count)])
        result = lax.dynamic_update_slice_in_dim(result, got, partner * place_len, place_dim)
    return result


def gather_members(block, axis):
    count = lax.axis_size(axis)
    me = lax.axis_index(axis)
    rows = block.shape[0]
    result = jnp.zeros((count * rows,) + block.shape[1:], block.dtype)
    result = lax.dynamic_update_slice_in_dim(result, block, me * rows, 0)
    for shift in range(1, count):
        partner = jnp.bitwise_xor(me, shift)
        got = lax.ppermute(block, axis, [(i, i ^ shift) for i in range(count)])
        result = lax.dynamic_update_slice_in_dim(result, got, partner * rows, 0)
    return result


def propagate_prior_state(
    haloed_state_grid,
    spreading_number,
    zonal_transport_ratio,
    meridional_transport_ratio,
    liquid_cell_flags,
):
    centre = haloed_state_grid[:, 1:-1, :]
    northern = haloed_state_grid[:, 2:, :]
    southern = haloed_state_grid[:, :-2, :]
    eastern = jnp.roll(centre, -1, axis=2)
    western = jnp.roll(centre, 1, axis=2)
    laplace = northern + southern + eastern + western - 4.0 * centre
    advect = (
        zonal_transport_ratio * (eastern - western) * 0.5
        + meridional_transport_ratio * (northern - southern) * 0.5
    )
    return liquid_cell_flags * (centre + spreading_number * laplace - advect)


def gram_kernel(
    picks_ref, meta_ref, window_ref, aux_ref, out_ref, table_ref, buf_ref, *, tb, tile_cols, grid_cols, members
):
    step = pl.program_id(0)
    base = step * (tb * OBS_TILE)
    width = table_ref.shape[1]

    @pl.when(step == 0)
    def _():
        def build(c, carry):
            start = pl.multiple_of(c * 128, 128)
            values = window_ref[:, pl.ds(start, 128)]
            mean = jnp.mean(values, axis=0, keepdims=True)
            extra = aux_ref[:, pl.ds(start, 128)]
            first = lax.broadcasted_iota(jnp.int32, extra.shape, 0) == 0
            extra = jnp.where(first, extra - mean, extra)
            rows = jnp.concatenate(
                [values - mean, extra, jnp.zeros((width - members - 8, 128), jnp.float32)], axis=0
            )
            table_ref[pl.ds(start, 128), :] = rows.T
            return carry

        lax.fori_loop(0, table_ref.shape[0] // 128, build, 0)


    unroll = 32

    def gather(j, carry):
        first = pl.multiple_of(j * unroll, unroll)
        at = base + first
        for u in range(unroll):
            idx = picks_ref[at + u]
            buf_ref[pl.ds(first + u, 1), :] = table_ref[pl.ds(idx, 1), :]
        return carry

    lax.fori_loop(0, tb * OBS_TILE // unroll, gather, 0)
    row_first = meta_ref[0]
    lane = lax.broadcasted_iota(jnp.int32, (OBS_TILE, width), 1)
    for t in range(tb):
        n = step * tb + t
        tile_row = jnp.full((OBS_TILE, 1), row_first + n // tile_cols, jnp.int32).astype(jnp.float32)
        tile_start = jnp.full((OBS_TILE, 1), TILE_COLS * (n % tile_cols), jnp.int32).astype(jnp.float32)
        blk = buf_ref[pl.ds(t * OBS_TILE, OBS_TILE), :]
        sig = blk[:, members + 1 : members + 2]
        orow = blk[:, members + 2 : members + 3]
        ocol = blk[:, members + 3 : members + 4]
        row_gap = orow - tile_row
        col_twice = 2.0 * ocol - 2.0 * tile_start - float(TILE_COLS - 1)
        col_twice = jnp.where(col_twice >= grid_cols, col_twice - 2.0 * grid_cols, col_twice)
        col_twice = jnp.where(col_twice < -grid_cols, col_twice + 2.0 * grid_cols, col_twice)
        col_gap = 0.5 * col_twice
        distance = row_gap * row_gap + col_gap * col_gap
        tapering = jnp.exp(-distance / (2.0 * LOC_RADIUS * LOC_RADIUS))
        weight = tapering / (sig * sig)
        rhs = jnp.where(lane <= members, blk, 0.0) * weight
        out_ref[t] = lax.dot_general(
            blk[:, :members],
            rhs,
            (((0,), (0,)), ((), ())),
            precision=highest,
            preferred_element_type=jnp.float32,
        )


def gram_and_forcing(window, aux, picks, row_first, tile_cols, grid_cols):
    tile_count = picks.shape[0]
    tb = 8 if tile_count % 8 == 0 else 1
    members, window_len = window.shape
    width = -(-(members + 8) // 128) * 128
    kernel = functools.partial(
        gram_kernel, tb=tb, tile_cols=tile_cols, grid_cols=grid_cols, members=members
    )
    meta = jnp.reshape(row_first, (1,)).astype(jnp.int32)
    return pl.pallas_call(
        kernel,
        grid_spec=pltpu.PrefetchScalarGridSpec(
            num_scalar_prefetch=2,
            grid=(tile_count // tb,),
            in_specs=[
                pl.BlockSpec((members, window_len), lambda s, p, m: (0, 0)),
                pl.BlockSpec(aux.shape, lambda s, p, m: (0, 0)),
            ],
            out_specs=pl.BlockSpec((tb, members, width), lambda s, p, m: (s, 0, 0)),
            scratch_shapes=[
                pltpu.VMEM((window_len, width), jnp.float32),
                pltpu.VMEM((tb * OBS_TILE, width), jnp.float32),
            ],
        ),
        out_shape=jax.ShapeDtypeStruct((tile_count, members, width), jnp.float32),
        compiler_params=pltpu.CompilerParams(dimension_semantics=("arbitrary",)),
    )(picks.reshape(-1), meta, window, aux)


def transform_of(moments, members):
    gram_matrix = moments[:, :, :members]
    forcing = moments[:, :, members]
    identity = jnp.eye(members, dtype=jnp.float32)
    system = gram_matrix + (members - 1.0) * identity
    frob_norm = jnp.sqrt(jnp.sum(system * system, axis=(1, 2)))
    iterate = system / frob_norm[:, None, None]
    factor = 1.5 * identity - 0.5 * iterate
    iterate = jnp.einsum("nij,njk->nik", iterate, factor, precision=lax.Precision.HIGH)
    inverse_root = factor
    for _ in range(1, NS_ITERS):
        factor = 1.5 * identity - 0.5 * jnp.einsum(
            "nij,njk->nik", inverse_root, iterate, precision=lax.Precision.HIGH
        )
        iterate = jnp.einsum("nij,njk->nik", iterate, factor, precision=lax.Precision.HIGH)
        inverse_root = jnp.einsum("nij,njk->nik", factor, inverse_root, precision=lax.Precision.HIGH)
    half_step = jnp.einsum("nkj,nj->nk", inverse_root, forcing, precision=highest)
    mean_weight = (
        jnp.einsum("nkj,nj->nk", inverse_root, half_step, precision=highest) / frob_norm[:, None]
    )
    return (
        jnp.sqrt(members - 1.0) * inverse_root / jnp.sqrt(frob_norm)[:, None, None]
        + mean_weight[:, :, None]
    )


def analysis_of(cells, transform):
    members, block_rows, block_cols = cells.shape
    tile_cells = cells.reshape(members, -1, TILE_COLS)
    centre_mean = jnp.mean(tile_cells, axis=0)
    spread = tile_cells - centre_mean
    analysis = centre_mean + jnp.einsum("jnt,njk->knt", spread, transform, precision=highest)
    return analysis.reshape(members, block_rows, block_cols)


def on_device(
    ensemble,
    spreading_number,
    zonal_transport_ratio,
    meridional_transport_ratio,
    ocean_mask,
    obs_loc,
    obs_value,
    obs_sigma,
    tile_obs,
):
    mem_dev, row_count, col_count = ensemble.shape
    liquid_cell_flags = ocean_mask.astype(jnp.float32)
    level_state_grid = liquid_cell_flags * ensemble
    for _ in range(2):
        haloed_state_grid = padded(level_state_grid, (("space", 1),), 1)
        level_state_grid = propagate_prior_state(
            haloed_state_grid,
            spreading_number,
            zonal_transport_ratio,
            meridional_transport_ratio,
            liquid_cell_flags,
        )
    space_index = lax.axis_index("space")
    member_index = lax.axis_index("member")
    obs_dev = obs_loc.shape[0] // lax.axis_size("space")
    flattened = level_state_grid.reshape(mem_dev, row_count * col_count)
    own_loc = lax.dynamic_slice_in_dim(obs_loc, space_index * obs_dev, obs_dev) - space_index * (
        row_count * col_count
    )
    own_obs = jnp.take(flattened, own_loc, axis=1)
    rimmed = padded(own_obs, (("space", 1),), obs_dev)
    window = gather_members(rimmed, "member")
    window_len = window.shape[1]

    def window_of(values, fill):
        rim = jnp.full((obs_dev,), fill, values.dtype)
        return lax.dynamic_slice_in_dim(
            jnp.concatenate([rim, values, rim]), space_index * obs_dev, window_len
        )

    window_loc = window_of(obs_loc, 0)
    aux = jnp.concatenate(
        [
            window_of(obs_value, 0.0)[None],
            window_of(obs_sigma, 1.0)[None],
            (window_loc // col_count).astype(jnp.float32)[None],
            (window_loc % col_count).astype(jnp.float32)[None],
            jnp.zeros((4, window_len), jnp.float32),
        ],
        axis=0,
    )
    first_obs = (space_index - 1) * obs_dev
    member_count = lax.axis_size("member")
    block_rows = row_count // member_count
    cell_block = exchange(
        level_state_grid.reshape(mem_dev, member_count, block_rows, col_count).transpose(
            1, 0, 2, 3
        ),
        "member",
        0,
        mem_dev,
    )
    tile_picks = lax.dynamic_slice_in_dim(tile_obs, member_index * block_rows, block_rows, 0)
    local_picks = jnp.clip(tile_picks - first_obs, 0, window_len - 1)
    row_first = space_index * row_count + member_index * block_rows
    members = window.shape[0]
    tile_cols = col_count // TILE_COLS
    moments = gram_and_forcing(
        window,
        aux,
        local_picks.reshape(block_rows * tile_cols, -1),
        row_first,
        tile_cols,
        col_count,
    )
    halves = 2 if tile_cols % 2 == 0 else 1
    part_cols = tile_cols // halves
    moments = moments.reshape(block_rows, tile_cols, members, moments.shape[-1])
    parts = []
    for half in range(halves):
        picked = moments[:, half * part_cols : (half + 1) * part_cols]
        transform = transform_of(picked.reshape(block_rows * part_cols, members, -1), members)
        lo, hi = half * part_cols * TILE_COLS, (half + 1) * part_cols * TILE_COLS
        updated = analysis_of(cell_block[:, :, lo:hi], transform)
        parts.append(
            exchange(
                updated.reshape(member_count, mem_dev, block_rows, hi - lo),
                "member",
                1,
                block_rows,
            )
        )
    result = jnp.concatenate(parts, axis=2) if halves > 1 else parts[0]
    return result


def solution(mesh):
    in_specs = (
        P("member", "space", None),
        P("space", None),
        P("space", None),
        P("space", None),
        P("space", None),
        P(),
        P(),
        P(),
        P("space", None, None),
    )
    out_specs = P("member", "space", None)

    return jax.shard_map(on_device, mesh=mesh, in_specs=in_specs, out_specs=out_specs, check_vma=False)
```

```python
import functools
import jax
import jax.numpy as jnp
from jax import lax
from jax.experimental import pallas as pl
from jax.experimental.pallas import tpu as pltpu
from jax.sharding import PartitionSpec as P


TILE_COLS = 128
OBS_TILE = 256
LOC_RADIUS = 96
NS_ITERS = 6


highest = lax.Precision.HIGHEST


def padded(cells, sides, width):
    for axis, dim in sides:
        count = lax.axis_size(axis)
        ends = count - 1
        head = lax.slice_in_dim(cells, 0, width, axis=dim)
        tail = lax.slice_in_dim(cells, cells.shape[dim] - width, cells.shape[dim], axis=dim)
        cells = jnp.concatenate(
            [
                lax.ppermute(tail, axis, [(i, (i + 1) % count) for i in range(ends)]),
                cells,
                lax.ppermute(head, axis, [((i + 1) % count, i) for i in range(ends)]),
            ],
            axis=dim,
        )
    return cells


def exchange(blocks, axis, place_dim, place_len):
    count = lax.axis_size(axis)
    me = lax.axis_index(axis)
    shape = list(blocks.shape[1:])
    shape[place_dim] *= count
    result = jnp.zeros(shape, blocks.dtype)
    result = lax.dynamic_update_slice_in_dim(
        result, lax.dynamic_index_in_dim(blocks, me, keepdims=False), me * place_len, place_dim
    )
    for shift in range(1, count):
        partner = jnp.bitwise_xor(me, shift)
        sent = lax.dynamic_index_in_dim(blocks, partner, keepdims=False)
        got = lax.ppermute(sent, axis, [(i, i ^ shift) for i in range(count)])
        result = lax.dynamic_update_slice_in_dim(result, got, partner * place_len, place_dim)
    return result


def gather_members(block, axis):
    count = lax.axis_size(axis)
    me = lax.axis_index(axis)
    rows = block.shape[0]
    result = jnp.zeros((count * rows,) + block.shape[1:], block.dtype)
    result = lax.dynamic_update_slice_in_dim(result, block, me * rows, 0)
    for shift in range(1, count):
        partner = jnp.bitwise_xor(me, shift)
        got = lax.ppermute(block, axis, [(i, i ^ shift) for i in range(count)])
        result = lax.dynamic_update_slice_in_dim(result, got, partner * rows, 0)
    return result


def propagate_prior_state(
    haloed_state_grid,
    spreading_number,
    zonal_transport_ratio,
    meridional_transport_ratio,
    liquid_cell_flags,
):
    centre = haloed_state_grid[:, 1:-1, :]
    northern = haloed_state_grid[:, 2:, :]
    southern = haloed_state_grid[:, :-2, :]
    eastern = jnp.roll(centre, -1, axis=2)
    western = jnp.roll(centre, 1, axis=2)
    laplace = northern + southern + eastern + western - 4.0 * centre
    advect = (
        zonal_transport_ratio * (eastern - western) * 0.5
        + meridional_transport_ratio * (northern - southern) * 0.5
    )
    return liquid_cell_flags * (centre + spreading_number * laplace - advect)


def gram_kernel(
    picks_ref, meta_ref, window_ref, aux_ref, out_ref, table_ref, buf_ref, *, tb, tile_cols, grid_cols, members
):
    step = pl.program_id(0)
    base = step * (tb * OBS_TILE)
    width = table_ref.shape[1]

    @pl.when(step == 0)
    def _():
        def build(c, carry):
            start = pl.multiple_of(c * 128, 128)
            values = window_ref[:, pl.ds(start, 128)]
            mean = jnp.mean(values, axis=0, keepdims=True)
            extra = aux_ref[:, pl.ds(start, 128)]
            first = lax.broadcasted_iota(jnp.int32, extra.shape, 0) == 0
            extra = jnp.where(first, extra - mean, extra)
            rows = jnp.concatenate(
                [values - mean, extra, jnp.zeros((width - members - 8, 128), jnp.float32)], axis=0
            )
            table_ref[pl.ds(start, 128), :] = rows.T
            return carry

        lax.fori_loop(0, table_ref.shape[0] // 128, build, 0)


    unroll = 32

    def gather(j, carry):
        first = pl.multiple_of(j * unroll, unroll)
        at = base + first
        for u in range(unroll):
            idx = picks_ref[at + u]
            buf_ref[pl.ds(first + u, 1), :] = table_ref[pl.ds(idx, 1), :]
        return carry

    lax.fori_loop(0, tb * OBS_TILE // unroll, gather, 0)
    row_first = meta_ref[0]
    for t in range(tb):
        n = step * tb + t
        tile_row = jnp.full((1, OBS_TILE), row_first + n // tile_cols, jnp.int32).astype(jnp.float32)
        tile_start = jnp.full((1, OBS_TILE), TILE_COLS * (n % tile_cols), jnp.int32).astype(
            jnp.float32
        )
        blk = buf_ref[pl.ds(t * OBS_TILE, OBS_TILE), :]
        blk_t = blk.T
        sig = blk_t[members + 1 : members + 2, :]
        orow = blk_t[members + 2 : members + 3, :]
        ocol = blk_t[members + 3 : members + 4, :]
        row_gap = orow - tile_row
        col_twice = 2.0 * ocol - 2.0 * tile_start - float(TILE_COLS - 1)
        col_twice = jnp.where(col_twice >= grid_cols, col_twice - 2.0 * grid_cols, col_twice)
        col_twice = jnp.where(col_twice < -grid_cols, col_twice + 2.0 * grid_cols, col_twice)
        col_gap = 0.5 * col_twice
        distance = row_gap * row_gap + col_gap * col_gap
        tapering = jnp.exp(-distance / (2.0 * LOC_RADIUS * LOC_RADIUS))
        weight = tapering / (sig * sig)
        lhs = blk_t[:members, :] * weight
        lhs_hi = lhs.astype(jnp.bfloat16)
        lhs_lo = (lhs - lhs_hi.astype(jnp.float32)).astype(jnp.bfloat16)
        rhs_hi = blk.astype(jnp.bfloat16)
        rhs_lo = (blk - rhs_hi.astype(jnp.float32)).astype(jnp.bfloat16)

        def product(x, y):
            return jnp.dot(x, y, preferred_element_type=jnp.float32)

        out_ref[t] = product(lhs_hi, rhs_hi) + (product(lhs_hi, rhs_lo) + product(lhs_lo, rhs_hi))


def gram_and_forcing(window, aux, picks, row_first, tile_cols, grid_cols):
    tile_count = picks.shape[0]
    tb = 8 if tile_count % 8 == 0 else 1
    members, window_len = window.shape
    width = -(-(members + 8) // 128) * 128
    kernel = functools.partial(
        gram_kernel, tb=tb, tile_cols=tile_cols, grid_cols=grid_cols, members=members
    )
    meta = jnp.reshape(row_first, (1,)).astype(jnp.int32)
    return pl.pallas_call(
        kernel,
        grid_spec=pltpu.PrefetchScalarGridSpec(
            num_scalar_prefetch=2,
            grid=(tile_count // tb,),
            in_specs=[
                pl.BlockSpec((members, window_len), lambda s, p, m: (0, 0)),
                pl.BlockSpec(aux.shape, lambda s, p, m: (0, 0)),
            ],
            out_specs=pl.BlockSpec((tb, members, width), lambda s, p, m: (s, 0, 0)),
            scratch_shapes=[
                pltpu.VMEM((window_len, width), jnp.float32),
                pltpu.VMEM((tb * OBS_TILE, width), jnp.float32),
            ],
        ),
        out_shape=jax.ShapeDtypeStruct((tile_count, members, width), jnp.float32),
        compiler_params=pltpu.CompilerParams(dimension_semantics=("arbitrary",)),
    )(picks.reshape(-1), meta, window, aux)


def transform_of(moments, members):
    gram_matrix = moments[:, :, :members]
    forcing = moments[:, :, members]
    identity = jnp.eye(members, dtype=jnp.float32)
    system = gram_matrix + (members - 1.0) * identity
    frob_norm = jnp.sqrt(jnp.sum(system * system, axis=(1, 2)))
    iterate = system / frob_norm[:, None, None]
    factor = 1.5 * identity - 0.5 * iterate
    iterate = jnp.einsum("nij,njk->nik", iterate, factor, precision=lax.Precision.HIGH)
    inverse_root = factor
    for _ in range(1, NS_ITERS):
        factor = 1.5 * identity - 0.5 * jnp.einsum(
            "nij,njk->nik", inverse_root, iterate, precision=lax.Precision.HIGH
        )
        iterate = jnp.einsum("nij,njk->nik", iterate, factor, precision=lax.Precision.HIGH)
        inverse_root = jnp.einsum("nij,njk->nik", factor, inverse_root, precision=lax.Precision.HIGH)
    half_step = jnp.einsum("nkj,nj->nk", inverse_root, forcing, precision=highest)
    mean_weight = (
        jnp.einsum("nkj,nj->nk", inverse_root, half_step, precision=highest) / frob_norm[:, None]
    )
    return (
        jnp.sqrt(members - 1.0) * inverse_root / jnp.sqrt(frob_norm)[:, None, None]
        + mean_weight[:, :, None]
    )


def analysis_of(cells, transform):
    members, block_rows, block_cols = cells.shape
    tile_cells = cells.reshape(members, -1, TILE_COLS)
    centre_mean = jnp.mean(tile_cells, axis=0)
    spread = tile_cells - centre_mean
    analysis = centre_mean + jnp.einsum("jnt,njk->knt", spread, transform, precision=highest)
    return analysis.reshape(members, block_rows, block_cols)


def on_device(
    ensemble,
    spreading_number,
    zonal_transport_ratio,
    meridional_transport_ratio,
    ocean_mask,
    obs_loc,
    obs_value,
    obs_sigma,
    tile_obs,
):
    mem_dev, row_count, col_count = ensemble.shape
    liquid_cell_flags = ocean_mask.astype(jnp.float32)
    level_state_grid = liquid_cell_flags * ensemble
    for _ in range(2):
        haloed_state_grid = padded(level_state_grid, (("space", 1),), 1)
        level_state_grid = propagate_prior_state(
            haloed_state_grid,
            spreading_number,
            zonal_transport_ratio,
            meridional_transport_ratio,
            liquid_cell_flags,
        )
    space_index = lax.axis_index("space")
    member_index = lax.axis_index("member")
    obs_dev = obs_loc.shape[0] // lax.axis_size("space")
    flattened = level_state_grid.reshape(mem_dev, row_count * col_count)
    own_loc = lax.dynamic_slice_in_dim(obs_loc, space_index * obs_dev, obs_dev) - space_index * (
        row_count * col_count
    )
    own_obs = jnp.take(flattened, own_loc, axis=1)
    rimmed = padded(own_obs, (("space", 1),), obs_dev)
    window = gather_members(rimmed, "member")
    window_len = window.shape[1]

    def window_of(values, fill):
        rim = jnp.full((obs_dev,), fill, values.dtype)
        return lax.dynamic_slice_in_dim(
            jnp.concatenate([rim, values, rim]), space_index * obs_dev, window_len
        )

    window_loc = window_of(obs_loc, 0)
    aux = jnp.concatenate(
        [
            window_of(obs_value, 0.0)[None],
            window_of(obs_sigma, 1.0)[None],
            (window_loc // col_count).astype(jnp.float32)[None],
            (window_loc % col_count).astype(jnp.float32)[None],
            jnp.zeros((4, window_len), jnp.float32),
        ],
        axis=0,
    )
    first_obs = (space_index - 1) * obs_dev
    member_count = lax.axis_size("member")
    block_rows = row_count // member_count
    cell_block = exchange(
        level_state_grid.reshape(mem_dev, member_count, block_rows, col_count).transpose(
            1, 0, 2, 3
        ),
        "member",
        0,
        mem_dev,
    )
    tile_picks = lax.dynamic_slice_in_dim(tile_obs, member_index * block_rows, block_rows, 0)
    local_picks = jnp.clip(tile_picks - first_obs, 0, window_len - 1)
    row_first = space_index * row_count + member_index * block_rows
    members = window.shape[0]
    tile_cols = col_count // TILE_COLS
    moments = gram_and_forcing(
        window,
        aux,
        local_picks.reshape(block_rows * tile_cols, -1),
        row_first,
        tile_cols,
        col_count,
    )
    halves = 2 if tile_cols % 2 == 0 else 1
    part_cols = tile_cols // halves
    moments = moments.reshape(block_rows, tile_cols, members, moments.shape[-1])
    parts = []
    for half in range(halves):
        picked = moments[:, half * part_cols : (half + 1) * part_cols]
        transform = transform_of(picked.reshape(block_rows * part_cols, members, -1), members)
        lo, hi = half * part_cols * TILE_COLS, (half + 1) * part_cols * TILE_COLS
        updated = analysis_of(cell_block[:, :, lo:hi], transform)
        parts.append(
            exchange(
                updated.reshape(member_count, mem_dev, block_rows, hi - lo),
                "member",
                1,
                block_rows,
            )
        )
    result = jnp.concatenate(parts, axis=2) if halves > 1 else parts[0]
    return result


def solution(mesh):
    in_specs = (
        P("member", "space", None),
        P("space", None),
        P("space", None),
        P("space", None),
        P("space", None),
        P(),
        P(),
        P(),
        P("space", None, None),
    )
    out_specs = P("member", "space", None)

    return jax.shard_map(on_device, mesh=mesh, in_specs=in_specs, out_specs=out_specs, check_vma=False)
```

```python
import functools
import jax
import jax.numpy as jnp
from jax import lax
from jax.experimental import pallas as pl
from jax.experimental.pallas import tpu as pltpu
from jax.sharding import PartitionSpec as P


TILE_COLS = 128
OBS_TILE = 256
LOC_RADIUS = 96
NS_ITERS = 6


highest = lax.Precision.HIGHEST


def padded(cells, sides, width):
    for axis, dim in sides:
        count = lax.axis_size(axis)
        ends = count - 1
        head = lax.slice_in_dim(cells, 0, width, axis=dim)
        tail = lax.slice_in_dim(cells, cells.shape[dim] - width, cells.shape[dim], axis=dim)
        cells = jnp.concatenate(
            [
                lax.ppermute(tail, axis, [(i, (i + 1) % count) for i in range(ends)]),
                cells,
                lax.ppermute(head, axis, [((i + 1) % count, i) for i in range(ends)]),
            ],
            axis=dim,
        )
    return cells


def exchange(blocks, axis, place_dim, place_len):
    count = lax.axis_size(axis)
    me = lax.axis_index(axis)
    shape = list(blocks.shape[1:])
    shape[place_dim] *= count
    result = jnp.zeros(shape, blocks.dtype)
    result = lax.dynamic_update_slice_in_dim(
        result, lax.dynamic_index_in_dim(blocks, me, keepdims=False), me * place_len, place_dim
    )
    for shift in range(1, count):
        partner = jnp.bitwise_xor(me, shift)
        sent = lax.dynamic_index_in_dim(blocks, partner, keepdims=False)
        got = lax.ppermute(sent, axis, [(i, i ^ shift) for i in range(count)])
        result = lax.dynamic_update_slice_in_dim(result, got, partner * place_len, place_dim)
    return result


def gather_members(block, axis):
    count = lax.axis_size(axis)
    me = lax.axis_index(axis)
    rows = block.shape[0]
    result = jnp.zeros((count * rows,) + block.shape[1:], block.dtype)
    result = lax.dynamic_update_slice_in_dim(result, block, me * rows, 0)
    for shift in range(1, count):
        partner = jnp.bitwise_xor(me, shift)
        got = lax.ppermute(block, axis, [(i, i ^ shift) for i in range(count)])
        result = lax.dynamic_update_slice_in_dim(result, got, partner * rows, 0)
    return result


def forecast_kernel(ens_ref, coef_ref, south_ref, north_ref, out_ref, state_ref, coef_ext_ref, step_ref):
    members, rows, cols = ens_ref.shape
    for k in range(4):
        plane, half = members + k // 2, k % 2
        coef_ext_ref[k, 0:1, :] = south_ref[plane, half : half + 1, :]
        coef_ext_ref[k, 1 : rows + 1, :] = coef_ref[k]
        coef_ext_ref[k, rows + 1 : rows + 2, :] = north_ref[plane, half : half + 1, :]

    def advance(centre, northern, southern, sea, spread, zonal, meridional):
        eastern = pltpu.roll(centre, cols - 1, 1)
        western = pltpu.roll(centre, 1, 1)
        laplace = northern + southern + eastern + western - 4.0 * centre
        advect = zonal * (eastern - western) * 0.5 + meridional * (northern - southern) * 0.5
        return sea * (centre + spread * laplace - advect)

    def member(m, carry):
        state_ref[0:2, :] = south_ref[m]
        state_ref[2 : rows + 2, :] = coef_ref[0] * ens_ref[m]
        state_ref[rows + 2 : rows + 4, :] = north_ref[m]
        step_ref[...] = advance(
            state_ref[1 : rows + 3, :],
            state_ref[2 : rows + 4, :],
            state_ref[0 : rows + 2, :],
            coef_ext_ref[0],
            coef_ext_ref[1],
            coef_ext_ref[2],
            coef_ext_ref[3],
        )
        out_ref[m] = advance(
            step_ref[1 : rows + 1, :],
            step_ref[2 : rows + 2, :],
            step_ref[0:rows, :],
            coef_ref[0],
            coef_ref[1],
            coef_ref[2],
            coef_ref[3],
        )
        return carry

    lax.fori_loop(0, members, member, 0)


def forecast(ensemble, sea, spreading_number, zonal_transport_ratio, meridional_transport_ratio):
    _, rows, cols = ensemble.shape
    coef = jnp.stack([sea, spreading_number, zonal_transport_ratio, meridional_transport_ratio])
    ends = lax.axis_size("space") - 1

    def edge(first, keep):
        state = coef[0, first : first + 2] * ensemble[:, first : first + 2]
        return jnp.concatenate([state, coef[:, keep].reshape(2, 2, cols)])

    south = lax.ppermute(edge(rows - 2, rows - 1), "space", [(i, i + 1) for i in range(ends)])
    north = lax.ppermute(edge(0, 0), "space", [(i + 1, i) for i in range(ends)])
    return pl.pallas_call(
        forecast_kernel,
        out_shape=jax.ShapeDtypeStruct(ensemble.shape, jnp.float32),
        in_specs=[pl.BlockSpec(memory_space=pltpu.VMEM)] * 4,
        out_specs=pl.BlockSpec(memory_space=pltpu.VMEM),
        scratch_shapes=[
            pltpu.VMEM((rows + 4, cols), jnp.float32),
            pltpu.VMEM((4, rows + 2, cols), jnp.float32),
            pltpu.VMEM((rows + 2, cols), jnp.float32),
        ],
    )(ensemble, coef, south, north)


def gram_kernel(
    picks_ref, meta_ref, window_ref, aux_ref, out_ref, table_ref, buf_ref, *, tb, tile_cols, grid_cols, members
):
    step = pl.program_id(0)
    base = step * (tb * OBS_TILE)
    width = table_ref.shape[1]

    @pl.when(step == 0)
    def _():
        def build(c, carry):
            start = pl.multiple_of(c * 128, 128)
            values = window_ref[:, pl.ds(start, 128)]
            mean = jnp.mean(values, axis=0, keepdims=True)
            extra = aux_ref[:, pl.ds(start, 128)]
            first = lax.broadcasted_iota(jnp.int32, extra.shape, 0) == 0
            extra = jnp.where(first, extra - mean, extra)
            rows = jnp.concatenate(
                [values - mean, extra, jnp.zeros((width - members - 8, 128), jnp.float32)], axis=0
            )
            table_ref[pl.ds(start, 128), :] = rows.T
            return carry

        lax.fori_loop(0, table_ref.shape[0] // 128, build, 0)


    unroll = 32

    def gather(j, carry):
        first = pl.multiple_of(j * unroll, unroll)
        at = base + first
        for u in range(unroll):
            idx = picks_ref[at + u]
            buf_ref[pl.ds(first + u, 1), :] = table_ref[pl.ds(idx, 1), :]
        return carry

    lax.fori_loop(0, tb * OBS_TILE // unroll, gather, 0)
    row_first = meta_ref[0]
    for t in range(tb):
        n = step * tb + t
        tile_row = jnp.full((1, OBS_TILE), row_first + n // tile_cols, jnp.int32).astype(jnp.float32)
        tile_start = jnp.full((1, OBS_TILE), TILE_COLS * (n % tile_cols), jnp.int32).astype(
            jnp.float32
        )
        blk = buf_ref[pl.ds(t * OBS_TILE, OBS_TILE), :]
        blk_t = blk.T
        sig = blk_t[members + 1 : members + 2, :]
        orow = blk_t[members + 2 : members + 3, :]
        ocol = blk_t[members + 3 : members + 4, :]
        row_gap = orow - tile_row
        col_twice = 2.0 * ocol - 2.0 * tile_start - float(TILE_COLS - 1)
        col_twice = jnp.where(col_twice >= grid_cols, col_twice - 2.0 * grid_cols, col_twice)
        col_twice = jnp.where(col_twice < -grid_cols, col_twice + 2.0 * grid_cols, col_twice)
        col_gap = 0.5 * col_twice
        distance = row_gap * row_gap + col_gap * col_gap
        tapering = jnp.exp(-distance / (2.0 * LOC_RADIUS * LOC_RADIUS))
        weight = tapering / (sig * sig)
        lhs = blk_t[:members, :] * weight
        lhs_hi = lhs.astype(jnp.bfloat16)
        lhs_lo = (lhs - lhs_hi.astype(jnp.float32)).astype(jnp.bfloat16)
        rhs_hi = blk.astype(jnp.bfloat16)
        rhs_lo = (blk - rhs_hi.astype(jnp.float32)).astype(jnp.bfloat16)

        def product(x, y):
            return jnp.dot(x, y, preferred_element_type=jnp.float32)

        out_ref[t] = product(lhs_hi, rhs_hi) + (product(lhs_hi, rhs_lo) + product(lhs_lo, rhs_hi))


def gram_and_forcing(window, aux, picks, row_first, tile_cols, grid_cols):
    tile_count = picks.shape[0]
    tb = 8 if tile_count % 8 == 0 else 1
    members, window_len = window.shape
    width = -(-(members + 8) // 128) * 128
    kernel = functools.partial(
        gram_kernel, tb=tb, tile_cols=tile_cols, grid_cols=grid_cols, members=members
    )
    meta = jnp.reshape(row_first, (1,)).astype(jnp.int32)
    return pl.pallas_call(
        kernel,
        grid_spec=pltpu.PrefetchScalarGridSpec(
            num_scalar_prefetch=2,
            grid=(tile_count // tb,),
            in_specs=[
                pl.BlockSpec((members, window_len), lambda s, p, m: (0, 0)),
                pl.BlockSpec(aux.shape, lambda s, p, m: (0, 0)),
            ],
            out_specs=pl.BlockSpec((tb, members, width), lambda s, p, m: (s, 0, 0)),
            scratch_shapes=[
                pltpu.VMEM((window_len, width), jnp.float32),
                pltpu.VMEM((tb * OBS_TILE, width), jnp.float32),
            ],
        ),
        out_shape=jax.ShapeDtypeStruct((tile_count, members, width), jnp.float32),
        compiler_params=pltpu.CompilerParams(dimension_semantics=("arbitrary",)),
    )(picks.reshape(-1), meta, window, aux)


def transform_of(moments, members):
    gram_matrix = moments[:, :, :members]
    forcing = moments[:, :, members]
    identity = jnp.eye(members, dtype=jnp.float32)
    system = gram_matrix + (members - 1.0) * identity
    frob_norm = jnp.sqrt(jnp.sum(system * system, axis=(1, 2)))
    iterate = system / frob_norm[:, None, None]
    factor = 1.5 * identity - 0.5 * iterate
    iterate = jnp.einsum("nij,njk->nik", iterate, factor, precision=lax.Precision.HIGH)
    inverse_root = factor
    for _ in range(1, NS_ITERS):
        factor = 1.5 * identity - 0.5 * jnp.einsum(
            "nij,njk->nik", inverse_root, iterate, precision=lax.Precision.HIGH
        )
        iterate = jnp.einsum("nij,njk->nik", iterate, factor, precision=lax.Precision.HIGH)
        inverse_root = jnp.einsum("nij,njk->nik", factor, inverse_root, precision=lax.Precision.HIGH)
    half_step = jnp.einsum("nkj,nj->nk", inverse_root, forcing, precision=highest)
    mean_weight = (
        jnp.einsum("nkj,nj->nk", inverse_root, half_step, precision=highest) / frob_norm[:, None]
    )
    return (
        jnp.sqrt(members - 1.0) * inverse_root / jnp.sqrt(frob_norm)[:, None, None]
        + mean_weight[:, :, None]
    )


def analysis_of(cells, transform):
    members, block_rows, block_cols = cells.shape
    tile_cells = cells.reshape(members, -1, TILE_COLS)
    centre_mean = jnp.mean(tile_cells, axis=0)
    spread = tile_cells - centre_mean
    analysis = centre_mean + jnp.einsum("jnt,njk->knt", spread, transform, precision=highest)
    return analysis.reshape(members, block_rows, block_cols)


def on_device(
    ensemble,
    spreading_number,
    zonal_transport_ratio,
    meridional_transport_ratio,
    ocean_mask,
    obs_loc,
    obs_value,
    obs_sigma,
    tile_obs,
):
    mem_dev, row_count, col_count = ensemble.shape
    liquid_cell_flags = ocean_mask.astype(jnp.float32)
    level_state_grid = forecast(
        ensemble,
        liquid_cell_flags,
        spreading_number,
        zonal_transport_ratio,
        meridional_transport_ratio,
    )
    space_index = lax.axis_index("space")
    member_index = lax.axis_index("member")
    obs_dev = obs_loc.shape[0] // lax.axis_size("space")
    flattened = level_state_grid.reshape(mem_dev, row_count * col_count)
    own_loc = lax.dynamic_slice_in_dim(obs_loc, space_index * obs_dev, obs_dev) - space_index * (
        row_count * col_count
    )
    own_obs = jnp.take(flattened, own_loc, axis=1)
    rimmed = padded(own_obs, (("space", 1),), obs_dev)
    window = gather_members(rimmed, "member")
    window_len = window.shape[1]

    def window_of(values, fill):
        rim = jnp.full((obs_dev,), fill, values.dtype)
        return lax.dynamic_slice_in_dim(
            jnp.concatenate([rim, values, rim]), space_index * obs_dev, window_len
        )

    window_loc = window_of(obs_loc, 0)
    aux = jnp.concatenate(
        [
            window_of(obs_value, 0.0)[None],
            window_of(obs_sigma, 1.0)[None],
            (window_loc // col_count).astype(jnp.float32)[None],
            (window_loc % col_count).astype(jnp.float32)[None],
            jnp.zeros((4, window_len), jnp.float32),
        ],
        axis=0,
    )
    first_obs = (space_index - 1) * obs_dev
    member_count = lax.axis_size("member")
    block_rows = row_count // member_count
    cell_block = exchange(
        level_state_grid.reshape(mem_dev, member_count, block_rows, col_count).transpose(
            1, 0, 2, 3
        ),
        "member",
        0,
        mem_dev,
    )
    tile_picks = lax.dynamic_slice_in_dim(tile_obs, member_index * block_rows, block_rows, 0)
    local_picks = jnp.clip(tile_picks - first_obs, 0, window_len - 1)
    row_first = space_index * row_count + member_index * block_rows
    members = window.shape[0]
    tile_cols = col_count // TILE_COLS
    moments = gram_and_forcing(
        window,
        aux,
        local_picks.reshape(block_rows * tile_cols, -1),
        row_first,
        tile_cols,
        col_count,
    )
    halves = 2 if tile_cols % 2 == 0 else 1
    part_cols = tile_cols // halves
    moments = moments.reshape(block_rows, tile_cols, members, moments.shape[-1])
    parts = []
    for half in range(halves):
        picked = moments[:, half * part_cols : (half + 1) * part_cols]
        transform = transform_of(picked.reshape(block_rows * part_cols, members, -1), members)
        lo, hi = half * part_cols * TILE_COLS, (half + 1) * part_cols * TILE_COLS
        updated = analysis_of(cell_block[:, :, lo:hi], transform)
        parts.append(
            exchange(
                updated.reshape(member_count, mem_dev, block_rows, hi - lo),
                "member",
                1,
                block_rows,
            )
        )
    result = jnp.concatenate(parts, axis=2) if halves > 1 else parts[0]
    return result


def solution(mesh):
    in_specs = (
        P("member", "space", None),
        P("space", None),
        P("space", None),
        P("space", None),
        P("space", None),
        P(),
        P(),
        P(),
        P("space", None, None),
    )
    out_specs = P("member", "space", None)

    return jax.shard_map(on_device, mesh=mesh, in_specs=in_specs, out_specs=out_specs, check_vma=False)
```

```python
import functools
import jax
import jax.numpy as jnp
from jax import lax
from jax.experimental import pallas as pl
from jax.experimental.pallas import tpu as pltpu
from jax.sharding import PartitionSpec as P


TILE_COLS = 128
OBS_TILE = 256
LOC_RADIUS = 96
NS_ITERS = 6


highest = lax.Precision.HIGHEST


def padded(cells, sides, width):
    for axis, dim in sides:
        count = lax.axis_size(axis)
        ends = count - 1
        head = lax.slice_in_dim(cells, 0, width, axis=dim)
        tail = lax.slice_in_dim(cells, cells.shape[dim] - width, cells.shape[dim], axis=dim)
        cells = jnp.concatenate(
            [
                lax.ppermute(tail, axis, [(i, (i + 1) % count) for i in range(ends)]),
                cells,
                lax.ppermute(head, axis, [((i + 1) % count, i) for i in range(ends)]),
            ],
            axis=dim,
        )
    return cells


def exchange(blocks, axis, place_dim, place_len):
    count = lax.axis_size(axis)
    me = lax.axis_index(axis)
    shape = list(blocks.shape[1:])
    shape[place_dim] *= count
    result = jnp.zeros(shape, blocks.dtype)
    result = lax.dynamic_update_slice_in_dim(
        result, lax.dynamic_index_in_dim(blocks, me, keepdims=False), me * place_len, place_dim
    )
    for shift in range(1, count):
        partner = jnp.bitwise_xor(me, shift)
        sent = lax.dynamic_index_in_dim(blocks, partner, keepdims=False)
        got = lax.ppermute(sent, axis, [(i, i ^ shift) for i in range(count)])
        result = lax.dynamic_update_slice_in_dim(result, got, partner * place_len, place_dim)
    return result


def gather_members(block, axis):
    count = lax.axis_size(axis)
    me = lax.axis_index(axis)
    rows = block.shape[0]
    result = jnp.zeros((count * rows,) + block.shape[1:], block.dtype)
    result = lax.dynamic_update_slice_in_dim(result, block, me * rows, 0)
    for shift in range(1, count):
        partner = jnp.bitwise_xor(me, shift)
        got = lax.ppermute(block, axis, [(i, i ^ shift) for i in range(count)])
        result = lax.dynamic_update_slice_in_dim(result, got, partner * rows, 0)
    return result


def forecast_kernel(ens_ref, coef_ref, south_ref, north_ref, out_ref, state_ref, coef_ext_ref, step_ref):
    members, rows, cols = ens_ref.shape
    for k in range(4):
        plane, half = members + k // 2, k % 2
        coef_ext_ref[k, 0:1, :] = south_ref[plane, half : half + 1, :]
        coef_ext_ref[k, 1 : rows + 1, :] = coef_ref[k]
        coef_ext_ref[k, rows + 1 : rows + 2, :] = north_ref[plane, half : half + 1, :]

    def advance(centre, northern, southern, sea, spread, zonal, meridional):
        eastern = pltpu.roll(centre, cols - 1, 1)
        western = pltpu.roll(centre, 1, 1)
        laplace = northern + southern + eastern + western - 4.0 * centre
        advect = zonal * (eastern - western) * 0.5 + meridional * (northern - southern) * 0.5
        return sea * (centre + spread * laplace - advect)

    def member(m, carry):
        state_ref[0:2, :] = south_ref[m]
        state_ref[2 : rows + 2, :] = coef_ref[0] * ens_ref[m]
        state_ref[rows + 2 : rows + 4, :] = north_ref[m]
        step_ref[...] = advance(
            state_ref[1 : rows + 3, :],
            state_ref[2 : rows + 4, :],
            state_ref[0 : rows + 2, :],
            coef_ext_ref[0],
            coef_ext_ref[1],
            coef_ext_ref[2],
            coef_ext_ref[3],
        )
        out_ref[m] = advance(
            step_ref[1 : rows + 1, :],
            step_ref[2 : rows + 2, :],
            step_ref[0:rows, :],
            coef_ref[0],
            coef_ref[1],
            coef_ref[2],
            coef_ref[3],
        )
        return carry

    lax.fori_loop(0, members, member, 0)


def forecast(ensemble, sea, spreading_number, zonal_transport_ratio, meridional_transport_ratio):
    _, rows, cols = ensemble.shape
    coef = jnp.stack([sea, spreading_number, zonal_transport_ratio, meridional_transport_ratio])
    ends = lax.axis_size("space") - 1

    def edge(first, keep):
        state = coef[0, first : first + 2] * ensemble[:, first : first + 2]
        return jnp.concatenate([state, coef[:, keep].reshape(2, 2, cols)])

    south = lax.ppermute(edge(rows - 2, rows - 1), "space", [(i, i + 1) for i in range(ends)])
    north = lax.ppermute(edge(0, 0), "space", [(i + 1, i) for i in range(ends)])
    return pl.pallas_call(
        forecast_kernel,
        out_shape=jax.ShapeDtypeStruct(ensemble.shape, jnp.float32),
        in_specs=[pl.BlockSpec(memory_space=pltpu.VMEM)] * 4,
        out_specs=pl.BlockSpec(memory_space=pltpu.VMEM),
        scratch_shapes=[
            pltpu.VMEM((rows + 4, cols), jnp.float32),
            pltpu.VMEM((4, rows + 2, cols), jnp.float32),
            pltpu.VMEM((rows + 2, cols), jnp.float32),
        ],
    )(ensemble, coef, south, north)


def gram_kernel(
    picks_ref, meta_ref, window_ref, aux_ref, out_ref, table_ref, buf_ref, *, tb, tile_cols, grid_cols, members
):
    step = pl.program_id(0)
    base = step * (tb * OBS_TILE)
    width = table_ref.shape[1]

    @pl.when(step == 0)
    def _():
        def build(c, carry):
            start = pl.multiple_of(c * 128, 128)
            values = window_ref[:, pl.ds(start, 128)]
            mean = jnp.mean(values, axis=0, keepdims=True)
            extra = aux_ref[:, pl.ds(start, 128)]
            first = lax.broadcasted_iota(jnp.int32, extra.shape, 0) == 0
            extra = jnp.where(first, extra - mean, extra)
            rows = jnp.concatenate(
                [values - mean, extra, jnp.zeros((width - members - 8, 128), jnp.float32)], axis=0
            )
            table_ref[pl.ds(start, 128), :] = rows.T
            return carry

        lax.fori_loop(0, table_ref.shape[0] // 128, build, 0)


    unroll = 32

    def gather(j, carry):
        first = pl.multiple_of(j * unroll, unroll)
        at = base + first
        for u in range(unroll):
            idx = picks_ref[at + u]
            buf_ref[pl.ds(first + u, 1), :] = table_ref[pl.ds(idx, 1), :]
        return carry

    lax.fori_loop(0, tb * OBS_TILE // unroll, gather, 0)
    row_first = meta_ref[0]
    for t in range(tb):
        n = step * tb + t
        tile_row = jnp.full((1, OBS_TILE), row_first + n // tile_cols, jnp.int32).astype(jnp.float32)
        tile_start = jnp.full((1, OBS_TILE), TILE_COLS * (n % tile_cols), jnp.int32).astype(
            jnp.float32
        )
        blk = buf_ref[pl.ds(t * OBS_TILE, OBS_TILE), :]
        blk_t = blk.T
        sig = blk_t[members + 1 : members + 2, :]
        orow = blk_t[members + 2 : members + 3, :]
        ocol = blk_t[members + 3 : members + 4, :]
        row_gap = orow - tile_row
        col_twice = 2.0 * ocol - 2.0 * tile_start - float(TILE_COLS - 1)
        col_twice = jnp.where(col_twice >= grid_cols, col_twice - 2.0 * grid_cols, col_twice)
        col_twice = jnp.where(col_twice < -grid_cols, col_twice + 2.0 * grid_cols, col_twice)
        col_gap = 0.5 * col_twice
        distance = row_gap * row_gap + col_gap * col_gap
        tapering = jnp.exp(-distance / (2.0 * LOC_RADIUS * LOC_RADIUS))
        weight = tapering / (sig * sig)
        lhs = blk_t[:members, :] * weight
        lhs_hi = lhs.astype(jnp.bfloat16)
        lhs_lo = (lhs - lhs_hi.astype(jnp.float32)).astype(jnp.bfloat16)
        rhs_hi = blk.astype(jnp.bfloat16)
        rhs_lo = (blk - rhs_hi.astype(jnp.float32)).astype(jnp.bfloat16)

        def product(x, y):
            return jnp.dot(x, y, preferred_element_type=jnp.float32)

        out_ref[t] = product(lhs_hi, rhs_hi) + (product(lhs_hi, rhs_lo) + product(lhs_lo, rhs_hi))


def gram_and_forcing(window, aux, picks, row_first, tile_cols, grid_cols):
    tile_count = picks.shape[0]
    tb = next(k for k in (16, 8, 1) if tile_count % k == 0)
    members, window_len = window.shape
    width = -(-(members + 8) // 128) * 128
    kernel = functools.partial(
        gram_kernel, tb=tb, tile_cols=tile_cols, grid_cols=grid_cols, members=members
    )
    meta = jnp.reshape(row_first, (1,)).astype(jnp.int32)
    return pl.pallas_call(
        kernel,
        grid_spec=pltpu.PrefetchScalarGridSpec(
            num_scalar_prefetch=2,
            grid=(tile_count // tb,),
            in_specs=[
                pl.BlockSpec((members, window_len), lambda s, p, m: (0, 0)),
                pl.BlockSpec(aux.shape, lambda s, p, m: (0, 0)),
            ],
            out_specs=pl.BlockSpec((tb, members, width), lambda s, p, m: (s, 0, 0)),
            scratch_shapes=[
                pltpu.VMEM((window_len, width), jnp.float32),
                pltpu.VMEM((tb * OBS_TILE, width), jnp.float32),
            ],
        ),
        out_shape=jax.ShapeDtypeStruct((tile_count, members, width), jnp.float32),
        compiler_params=pltpu.CompilerParams(dimension_semantics=("arbitrary",)),
    )(picks.reshape(-1), meta, window, aux)


def transform_of(moments, members):
    gram_matrix = moments[:, :, :members]
    forcing = moments[:, :, members]
    identity = jnp.eye(members, dtype=jnp.float32)
    system = gram_matrix + (members - 1.0) * identity
    frob_norm = jnp.sqrt(jnp.sum(system * system, axis=(1, 2)))
    iterate = system / frob_norm[:, None, None]
    factor = 1.5 * identity - 0.5 * iterate
    iterate = jnp.einsum("nij,njk->nik", iterate, factor, precision=lax.Precision.HIGH)
    inverse_root = factor
    for _ in range(1, NS_ITERS):
        factor = 1.5 * identity - 0.5 * jnp.einsum(
            "nij,njk->nik", inverse_root, iterate, precision=lax.Precision.HIGH
        )
        iterate = jnp.einsum("nij,njk->nik", iterate, factor, precision=lax.Precision.HIGH)
        inverse_root = jnp.einsum("nij,njk->nik", factor, inverse_root, precision=lax.Precision.HIGH)
    half_step = jnp.einsum("nkj,nj->nk", inverse_root, forcing, precision=highest)
    mean_weight = (
        jnp.einsum("nkj,nj->nk", inverse_root, half_step, precision=highest) / frob_norm[:, None]
    )
    return (
        jnp.sqrt(members - 1.0) * inverse_root / jnp.sqrt(frob_norm)[:, None, None]
        + mean_weight[:, :, None]
    )


def analysis_of(cells, transform):
    members, block_rows, block_cols = cells.shape
    tile_cells = cells.reshape(members, -1, TILE_COLS)
    centre_mean = jnp.mean(tile_cells, axis=0)
    spread = tile_cells - centre_mean
    analysis = centre_mean + jnp.einsum("jnt,njk->knt", spread, transform, precision=highest)
    return analysis.reshape(members, block_rows, block_cols)


def on_device(
    ensemble,
    spreading_number,
    zonal_transport_ratio,
    meridional_transport_ratio,
    ocean_mask,
    obs_loc,
    obs_value,
    obs_sigma,
    tile_obs,
):
    mem_dev, row_count, col_count = ensemble.shape
    liquid_cell_flags = ocean_mask.astype(jnp.float32)
    level_state_grid = forecast(
        ensemble,
        liquid_cell_flags,
        spreading_number,
        zonal_transport_ratio,
        meridional_transport_ratio,
    )
    space_index = lax.axis_index("space")
    member_index = lax.axis_index("member")
    obs_dev = obs_loc.shape[0] // lax.axis_size("space")
    flattened = level_state_grid.reshape(mem_dev, row_count * col_count)
    own_loc = lax.dynamic_slice_in_dim(obs_loc, space_index * obs_dev, obs_dev) - space_index * (
        row_count * col_count
    )
    own_obs = jnp.take(flattened, own_loc, axis=1)
    window = padded(gather_members(own_obs, "member"), (("space", 1),), obs_dev)
    window_len = window.shape[1]

    def window_of(values, fill):
        rim = jnp.full((obs_dev,), fill, values.dtype)
        return lax.dynamic_slice_in_dim(
            jnp.concatenate([rim, values, rim]), space_index * obs_dev, window_len
        )

    window_loc = window_of(obs_loc, 0)
    aux = jnp.concatenate(
        [
            window_of(obs_value, 0.0)[None],
            window_of(obs_sigma, 1.0)[None],
            (window_loc // col_count).astype(jnp.float32)[None],
            (window_loc % col_count).astype(jnp.float32)[None],
            jnp.zeros((4, window_len), jnp.float32),
        ],
        axis=0,
    )
    first_obs = (space_index - 1) * obs_dev
    member_count = lax.axis_size("member")
    block_rows = row_count // member_count
    cell_block = exchange(
        level_state_grid.reshape(mem_dev, member_count, block_rows, col_count).transpose(
            1, 0, 2, 3
        ),
        "member",
        0,
        mem_dev,
    )
    tile_picks = lax.dynamic_slice_in_dim(tile_obs, member_index * block_rows, block_rows, 0)
    local_picks = jnp.clip(tile_picks - first_obs, 0, window_len - 1)
    row_first = space_index * row_count + member_index * block_rows
    members = window.shape[0]
    tile_cols = col_count // TILE_COLS
    moments = gram_and_forcing(
        window,
        aux,
        local_picks.reshape(block_rows * tile_cols, -1),
        row_first,
        tile_cols,
        col_count,
    )
    halves = 2 if tile_cols % 2 == 0 else 1
    part_cols = tile_cols // halves
    moments = moments.reshape(block_rows, tile_cols, members, moments.shape[-1])
    parts = []
    for half in range(halves):
        picked = moments[:, half * part_cols : (half + 1) * part_cols]
        transform = transform_of(picked.reshape(block_rows * part_cols, members, -1), members)
        lo, hi = half * part_cols * TILE_COLS, (half + 1) * part_cols * TILE_COLS
        updated = analysis_of(cell_block[:, :, lo:hi], transform)
        parts.append(
            exchange(
                updated.reshape(member_count, mem_dev, block_rows, hi - lo),
                "member",
                1,
                block_rows,
            )
        )
    result = jnp.concatenate(parts, axis=2) if halves > 1 else parts[0]
    return result


def solution(mesh):
    in_specs = (
        P("member", "space", None),
        P("space", None),
        P("space", None),
        P("space", None),
        P("space", None),
        P(),
        P(),
        P(),
        P("space", None, None),
    )
    out_specs = P("member", "space", None)

    return jax.shard_map(on_device, mesh=mesh, in_specs=in_specs, out_specs=out_specs, check_vma=False)
```

```python
import functools
import jax
import jax.numpy as jnp
from jax import lax
from jax.experimental import pallas as pl
from jax.experimental.pallas import tpu as pltpu
from jax.sharding import PartitionSpec as P


TILE_COLS = 128
OBS_TILE = 256
LOC_RADIUS = 96
NS_ITERS = 6


highest = lax.Precision.HIGHEST


def padded(cells, sides, width):
    for axis, dim in sides:
        count = lax.axis_size(axis)
        ends = count - 1
        head = lax.slice_in_dim(cells, 0, width, axis=dim)
        tail = lax.slice_in_dim(cells, cells.shape[dim] - width, cells.shape[dim], axis=dim)
        cells = jnp.concatenate(
            [
                lax.ppermute(tail, axis, [(i, (i + 1) % count) for i in range(ends)]),
                cells,
                lax.ppermute(head, axis, [((i + 1) % count, i) for i in range(ends)]),
            ],
            axis=dim,
        )
    return cells


def exchange(blocks, axis, place_dim, place_len):
    count = lax.axis_size(axis)
    me = lax.axis_index(axis)
    shape = list(blocks.shape[1:])
    shape[place_dim] *= count
    result = jnp.zeros(shape, blocks.dtype)
    result = lax.dynamic_update_slice_in_dim(
        result, lax.dynamic_index_in_dim(blocks, me, keepdims=False), me * place_len, place_dim
    )
    for shift in range(1, count):
        partner = jnp.bitwise_xor(me, shift)
        sent = lax.dynamic_index_in_dim(blocks, partner, keepdims=False)
        got = lax.ppermute(sent, axis, [(i, i ^ shift) for i in range(count)])
        result = lax.dynamic_update_slice_in_dim(result, got, partner * place_len, place_dim)
    return result


def scatter_back(result, blocks, axis, row_len, col_first):
    count = lax.axis_size(axis)
    me = lax.axis_index(axis)
    own = lax.dynamic_index_in_dim(blocks, me, keepdims=False)
    result = lax.dynamic_update_slice(result, own, (0, me * row_len, col_first))
    for shift in range(1, count):
        partner = jnp.bitwise_xor(me, shift)
        sent = lax.dynamic_index_in_dim(blocks, partner, keepdims=False)
        got = lax.ppermute(sent, axis, [(i, i ^ shift) for i in range(count)])
        result = lax.dynamic_update_slice(result, got, (0, partner * row_len, col_first))
    return result


def gather_members(block, axis):
    count = lax.axis_size(axis)
    me = lax.axis_index(axis)
    rows = block.shape[0]
    result = jnp.zeros((count * rows,) + block.shape[1:], block.dtype)
    result = lax.dynamic_update_slice_in_dim(result, block, me * rows, 0)
    for shift in range(1, count):
        partner = jnp.bitwise_xor(me, shift)
        got = lax.ppermute(block, axis, [(i, i ^ shift) for i in range(count)])
        result = lax.dynamic_update_slice_in_dim(result, got, partner * rows, 0)
    return result


def forecast_kernel(ens_ref, coef_ref, south_ref, north_ref, out_ref, state_ref, coef_ext_ref, step_ref):
    members, rows, cols = ens_ref.shape
    for k in range(4):
        plane, half = members + k // 2, k % 2
        coef_ext_ref[k, 0:1, :] = south_ref[plane, half : half + 1, :]
        coef_ext_ref[k, 1 : rows + 1, :] = coef_ref[k]
        coef_ext_ref[k, rows + 1 : rows + 2, :] = north_ref[plane, half : half + 1, :]

    def advance(centre, northern, southern, sea, spread, zonal, meridional):
        eastern = pltpu.roll(centre, cols - 1, 1)
        western = pltpu.roll(centre, 1, 1)
        laplace = northern + southern + eastern + western - 4.0 * centre
        advect = zonal * (eastern - western) * 0.5 + meridional * (northern - southern) * 0.5
        return sea * (centre + spread * laplace - advect)

    def member(m, carry):
        state_ref[0:2, :] = south_ref[m]
        state_ref[2 : rows + 2, :] = coef_ref[0] * ens_ref[m]
        state_ref[rows + 2 : rows + 4, :] = north_ref[m]
        step_ref[...] = advance(
            state_ref[1 : rows + 3, :],
            state_ref[2 : rows + 4, :],
            state_ref[0 : rows + 2, :],
            coef_ext_ref[0],
            coef_ext_ref[1],
            coef_ext_ref[2],
            coef_ext_ref[3],
        )
        out_ref[m] = advance(
            step_ref[1 : rows + 1, :],
            step_ref[2 : rows + 2, :],
            step_ref[0:rows, :],
            coef_ref[0],
            coef_ref[1],
            coef_ref[2],
            coef_ref[3],
        )
        return carry

    lax.fori_loop(0, members, member, 0)


def forecast(ensemble, sea, spreading_number, zonal_transport_ratio, meridional_transport_ratio):
    _, rows, cols = ensemble.shape
    coef = jnp.stack([sea, spreading_number, zonal_transport_ratio, meridional_transport_ratio])
    ends = lax.axis_size("space") - 1

    def edge(first, keep):
        state = coef[0, first : first + 2] * ensemble[:, first : first + 2]
        return jnp.concatenate([state, coef[:, keep].reshape(2, 2, cols)])

    south = lax.ppermute(edge(rows - 2, rows - 1), "space", [(i, i + 1) for i in range(ends)])
    north = lax.ppermute(edge(0, 0), "space", [(i + 1, i) for i in range(ends)])
    return pl.pallas_call(
        forecast_kernel,
        out_shape=jax.ShapeDtypeStruct(ensemble.shape, jnp.float32),
        in_specs=[pl.BlockSpec(memory_space=pltpu.VMEM)] * 4,
        out_specs=pl.BlockSpec(memory_space=pltpu.VMEM),
        scratch_shapes=[
            pltpu.VMEM((rows + 4, cols), jnp.float32),
            pltpu.VMEM((4, rows + 2, cols), jnp.float32),
            pltpu.VMEM((rows + 2, cols), jnp.float32),
        ],
    )(ensemble, coef, south, north)


def gram_kernel(
    picks_ref, meta_ref, window_ref, aux_ref, out_ref, table_ref, buf_ref, *, tb, tile_cols, grid_cols, members
):
    step = pl.program_id(0)
    base = step * (tb * OBS_TILE)
    width = table_ref.shape[1]

    @pl.when(step == 0)
    def _():
        def build(c, carry):
            start = pl.multiple_of(c * 128, 128)
            values = window_ref[:, pl.ds(start, 128)]
            mean = jnp.mean(values, axis=0, keepdims=True)
            extra = aux_ref[:, pl.ds(start, 128)]
            first = lax.broadcasted_iota(jnp.int32, extra.shape, 0) == 0
            extra = jnp.where(first, extra - mean, extra)
            rows = jnp.concatenate(
                [values - mean, extra, jnp.zeros((width - members - 8, 128), jnp.float32)], axis=0
            )
            table_ref[pl.ds(start, 128), :] = rows.T
            return carry

        lax.fori_loop(0, table_ref.shape[0] // 128, build, 0)


    unroll = 32

    def gather(j, carry):
        first = pl.multiple_of(j * unroll, unroll)
        at = base + first
        for u in range(unroll):
            idx = picks_ref[at + u]
            buf_ref[pl.ds(first + u, 1), :] = table_ref[pl.ds(idx, 1), :]
        return carry

    lax.fori_loop(0, tb * OBS_TILE // unroll, gather, 0)
    row_first = meta_ref[0]
    for t in range(tb):
        n = step * tb + t
        tile_row = jnp.full((1, OBS_TILE), row_first + n // tile_cols, jnp.int32).astype(jnp.float32)
        tile_start = jnp.full((1, OBS_TILE), TILE_COLS * (n % tile_cols), jnp.int32).astype(
            jnp.float32
        )
        blk = buf_ref[pl.ds(t * OBS_TILE, OBS_TILE), :]
        blk_t = blk.T
        sig = blk_t[members + 1 : members + 2, :]
        orow = blk_t[members + 2 : members + 3, :]
        ocol = blk_t[members + 3 : members + 4, :]
        row_gap = orow - tile_row
        col_twice = 2.0 * ocol - 2.0 * tile_start - float(TILE_COLS - 1)
        col_twice = jnp.where(col_twice >= grid_cols, col_twice - 2.0 * grid_cols, col_twice)
        col_twice = jnp.where(col_twice < -grid_cols, col_twice + 2.0 * grid_cols, col_twice)
        col_gap = 0.5 * col_twice
        distance = row_gap * row_gap + col_gap * col_gap
        tapering = jnp.exp(-distance / (2.0 * LOC_RADIUS * LOC_RADIUS))
        weight = tapering / (sig * sig)
        lhs = blk_t[:members, :] * weight
        lhs_hi = lhs.astype(jnp.bfloat16)
        lhs_lo = (lhs - lhs_hi.astype(jnp.float32)).astype(jnp.bfloat16)
        rhs_hi = blk.astype(jnp.bfloat16)
        rhs_lo = (blk - rhs_hi.astype(jnp.float32)).astype(jnp.bfloat16)

        def product(x, y):
            return jnp.dot(x, y, preferred_element_type=jnp.float32)

        out_ref[t] = product(lhs_hi, rhs_hi) + (product(lhs_hi, rhs_lo) + product(lhs_lo, rhs_hi))


def gram_and_forcing(window, aux, picks, row_first, tile_cols, grid_cols):
    tile_count = picks.shape[0]
    tb = next(k for k in (16, 8, 1) if tile_count % k == 0)
    members, window_len = window.shape
    width = -(-(members + 8) // 128) * 128
    kernel = functools.partial(
        gram_kernel, tb=tb, tile_cols=tile_cols, grid_cols=grid_cols, members=members
    )
    meta = jnp.reshape(row_first, (1,)).astype(jnp.int32)
    return pl.pallas_call(
        kernel,
        grid_spec=pltpu.PrefetchScalarGridSpec(
            num_scalar_prefetch=2,
            grid=(tile_count // tb,),
            in_specs=[
                pl.BlockSpec((members, window_len), lambda s, p, m: (0, 0)),
                pl.BlockSpec(aux.shape, lambda s, p, m: (0, 0)),
            ],
            out_specs=pl.BlockSpec((tb, members, width), lambda s, p, m: (s, 0, 0)),
            scratch_shapes=[
                pltpu.VMEM((window_len, width), jnp.float32),
                pltpu.VMEM((tb * OBS_TILE, width), jnp.float32),
            ],
        ),
        out_shape=jax.ShapeDtypeStruct((tile_count, members, width), jnp.float32),
        compiler_params=pltpu.CompilerParams(dimension_semantics=("arbitrary",)),
    )(picks.reshape(-1), meta, window, aux)


def transform_of(moments, members):
    gram_matrix = moments[:, :, :members]
    forcing = moments[:, :, members]
    identity = jnp.eye(members, dtype=jnp.float32)
    system = gram_matrix + (members - 1.0) * identity
    frob_norm = jnp.sqrt(jnp.sum(system * system, axis=(1, 2)))
    iterate = system / frob_norm[:, None, None]
    factor = 1.5 * identity - 0.5 * iterate
    iterate = jnp.einsum("nij,njk->nik", iterate, factor, precision=lax.Precision.HIGH)
    inverse_root = factor
    for _ in range(1, NS_ITERS):
        factor = 1.5 * identity - 0.5 * jnp.einsum(
            "nij,njk->nik", inverse_root, iterate, precision=lax.Precision.HIGH
        )
        iterate = jnp.einsum("nij,njk->nik", iterate, factor, precision=lax.Precision.HIGH)
        inverse_root = jnp.einsum("nij,njk->nik", factor, inverse_root, precision=lax.Precision.HIGH)
    half_step = jnp.einsum("nkj,nj->nk", inverse_root, forcing, precision=highest)
    mean_weight = (
        jnp.einsum("nkj,nj->nk", inverse_root, half_step, precision=highest) / frob_norm[:, None]
    )
    return (
        jnp.sqrt(members - 1.0) * inverse_root / jnp.sqrt(frob_norm)[:, None, None]
        + mean_weight[:, :, None]
    )


def analysis_of(cells, transform):
    members, block_rows, block_cols = cells.shape
    tile_cells = cells.reshape(members, -1, TILE_COLS)
    centre_mean = jnp.mean(tile_cells, axis=0)
    spread = tile_cells - centre_mean
    analysis = centre_mean + jnp.einsum("jnt,njk->knt", spread, transform, precision=highest)
    return analysis.reshape(members, block_rows, block_cols)


def on_device(
    ensemble,
    spreading_number,
    zonal_transport_ratio,
    meridional_transport_ratio,
    ocean_mask,
    obs_loc,
    obs_value,
    obs_sigma,
    tile_obs,
):
    mem_dev, row_count, col_count = ensemble.shape
    liquid_cell_flags = ocean_mask.astype(jnp.float32)
    level_state_grid = forecast(
        ensemble,
        liquid_cell_flags,
        spreading_number,
        zonal_transport_ratio,
        meridional_transport_ratio,
    )
    space_index = lax.axis_index("space")
    member_index = lax.axis_index("member")
    obs_dev = obs_loc.shape[0] // lax.axis_size("space")
    flattened = level_state_grid.reshape(mem_dev, row_count * col_count)
    own_loc = lax.dynamic_slice_in_dim(obs_loc, space_index * obs_dev, obs_dev) - space_index * (
        row_count * col_count
    )
    own_obs = jnp.take(flattened, own_loc, axis=1)
    window = padded(gather_members(own_obs, "member"), (("space", 1),), obs_dev)
    window_len = window.shape[1]

    def window_of(values, fill):
        rim = jnp.full((obs_dev,), fill, values.dtype)
        return lax.dynamic_slice_in_dim(
            jnp.concatenate([rim, values, rim]), space_index * obs_dev, window_len
        )

    window_loc = window_of(obs_loc, 0)
    aux = jnp.concatenate(
        [
            window_of(obs_value, 0.0)[None],
            window_of(obs_sigma, 1.0)[None],
            (window_loc // col_count).astype(jnp.float32)[None],
            (window_loc % col_count).astype(jnp.float32)[None],
            jnp.zeros((4, window_len), jnp.float32),
        ],
        axis=0,
    )
    first_obs = (space_index - 1) * obs_dev
    member_count = lax.axis_size("member")
    block_rows = row_count // member_count
    cell_block = exchange(
        level_state_grid.reshape(mem_dev, member_count, block_rows, col_count).transpose(
            1, 0, 2, 3
        ),
        "member",
        0,
        mem_dev,
    )
    tile_picks = lax.dynamic_slice_in_dim(tile_obs, member_index * block_rows, block_rows, 0)
    local_picks = jnp.clip(tile_picks - first_obs, 0, window_len - 1)
    row_first = space_index * row_count + member_index * block_rows
    members = window.shape[0]
    tile_cols = col_count // TILE_COLS
    moments = gram_and_forcing(
        window,
        aux,
        local_picks.reshape(block_rows * tile_cols, -1),
        row_first,
        tile_cols,
        col_count,
    )
    halves = 2 if tile_cols % 2 == 0 else 1
    part_cols = tile_cols // halves
    moments = moments.reshape(block_rows, tile_cols, members, moments.shape[-1])
    result = jnp.zeros((mem_dev, row_count, col_count), jnp.float32)
    for half in range(halves):
        picked = moments[:, half * part_cols : (half + 1) * part_cols]
        transform = transform_of(picked.reshape(block_rows * part_cols, members, -1), members)
        lo, hi = half * part_cols * TILE_COLS, (half + 1) * part_cols * TILE_COLS
        updated = analysis_of(cell_block[:, :, lo:hi], transform)
        result = scatter_back(
            result,
            updated.reshape(member_count, mem_dev, block_rows, hi - lo),
            "member",
            block_rows,
            lo,
        )
    return result


def solution(mesh):
    in_specs = (
        P("member", "space", None),
        P("space", None),
        P("space", None),
        P("space", None),
        P("space", None),
        P(),
        P(),
        P(),
        P("space", None, None),
    )
    out_specs = P("member", "space", None)

    return jax.shard_map(on_device, mesh=mesh, in_specs=in_specs, out_specs=out_specs, check_vma=False)
```

```python
import functools
import jax
import jax.numpy as jnp
from jax import lax
from jax.experimental import pallas as pl
from jax.experimental.pallas import tpu as pltpu
from jax.sharding import PartitionSpec as P


TILE_COLS = 128
OBS_TILE = 256
LOC_RADIUS = 96
NS_ITERS = 6


highest = lax.Precision.HIGHEST


def padded(cells, sides, width):
    for axis, dim in sides:
        count = lax.axis_size(axis)
        ends = count - 1
        head = lax.slice_in_dim(cells, 0, width, axis=dim)
        tail = lax.slice_in_dim(cells, cells.shape[dim] - width, cells.shape[dim], axis=dim)
        cells = jnp.concatenate(
            [
                lax.ppermute(tail, axis, [(i, (i + 1) % count) for i in range(ends)]),
                cells,
                lax.ppermute(head, axis, [((i + 1) % count, i) for i in range(ends)]),
            ],
            axis=dim,
        )
    return cells


def exchange(blocks, axis, place_dim, place_len):
    count = lax.axis_size(axis)
    me = lax.axis_index(axis)
    shape = list(blocks.shape[1:])
    shape[place_dim] *= count
    result = jnp.zeros(shape, blocks.dtype)
    result = lax.dynamic_update_slice_in_dim(
        result, lax.dynamic_index_in_dim(blocks, me, keepdims=False), me * place_len, place_dim
    )
    for shift in range(1, count):
        partner = jnp.bitwise_xor(me, shift)
        sent = lax.dynamic_index_in_dim(blocks, partner, keepdims=False)
        got = lax.ppermute(sent, axis, [(i, i ^ shift) for i in range(count)])
        result = lax.dynamic_update_slice_in_dim(result, got, partner * place_len, place_dim)
    return result


def gather_members(block, axis):
    count = lax.axis_size(axis)
    me = lax.axis_index(axis)
    rows = block.shape[0]
    result = jnp.zeros((count * rows,) + block.shape[1:], block.dtype)
    result = lax.dynamic_update_slice_in_dim(result, block, me * rows, 0)
    for shift in range(1, count):
        partner = jnp.bitwise_xor(me, shift)
        got = lax.ppermute(block, axis, [(i, i ^ shift) for i in range(count)])
        result = lax.dynamic_update_slice_in_dim(result, got, partner * rows, 0)
    return result


def forecast_kernel(ens_ref, coef_ref, south_ref, north_ref, out_ref, state_ref, coef_ext_ref, step_ref):
    members, rows, cols = ens_ref.shape
    for k in range(4):
        plane, half = members + k // 2, k % 2
        coef_ext_ref[k, 0:1, :] = south_ref[plane, half : half + 1, :]
        coef_ext_ref[k, 1 : rows + 1, :] = coef_ref[k]
        coef_ext_ref[k, rows + 1 : rows + 2, :] = north_ref[plane, half : half + 1, :]

    def advance(centre, northern, southern, sea, spread, zonal, meridional):
        eastern = pltpu.roll(centre, cols - 1, 1)
        western = pltpu.roll(centre, 1, 1)
        laplace = northern + southern + eastern + western - 4.0 * centre
        advect = zonal * (eastern - western) * 0.5 + meridional * (northern - southern) * 0.5
        return sea * (centre + spread * laplace - advect)

    def member(m, carry):
        state_ref[0:2, :] = south_ref[m]
        state_ref[2 : rows + 2, :] = coef_ref[0] * ens_ref[m]
        state_ref[rows + 2 : rows + 4, :] = north_ref[m]
        step_ref[...] = advance(
            state_ref[1 : rows + 3, :],
            state_ref[2 : rows + 4, :],
            state_ref[0 : rows + 2, :],
            coef_ext_ref[0],
            coef_ext_ref[1],
            coef_ext_ref[2],
            coef_ext_ref[3],
        )
        out_ref[m] = advance(
            step_ref[1 : rows + 1, :],
            step_ref[2 : rows + 2, :],
            step_ref[0:rows, :],
            coef_ref[0],
            coef_ref[1],
            coef_ref[2],
            coef_ref[3],
        )
        return carry

    lax.fori_loop(0, members, member, 0)


def forecast(ensemble, sea, spreading_number, zonal_transport_ratio, meridional_transport_ratio):
    _, rows, cols = ensemble.shape
    coef = jnp.stack([sea, spreading_number, zonal_transport_ratio, meridional_transport_ratio])
    ends = lax.axis_size("space") - 1

    def edge(first, keep):
        state = coef[0, first : first + 2] * ensemble[:, first : first + 2]
        return jnp.concatenate([state, coef[:, keep].reshape(2, 2, cols)])

    south = lax.ppermute(edge(rows - 2, rows - 1), "space", [(i, i + 1) for i in range(ends)])
    north = lax.ppermute(edge(0, 0), "space", [(i + 1, i) for i in range(ends)])
    return pl.pallas_call(
        forecast_kernel,
        out_shape=jax.ShapeDtypeStruct(ensemble.shape, jnp.float32),
        in_specs=[pl.BlockSpec(memory_space=pltpu.VMEM)] * 4,
        out_specs=pl.BlockSpec(memory_space=pltpu.VMEM),
        scratch_shapes=[
            pltpu.VMEM((rows + 4, cols), jnp.float32),
            pltpu.VMEM((4, rows + 2, cols), jnp.float32),
            pltpu.VMEM((rows + 2, cols), jnp.float32),
        ],
    )(ensemble, coef, south, north)


def gram_kernel(
    picks_ref, meta_ref, window_ref, aux_ref, out_ref, table_ref, buf_ref, *, tb, tile_cols, grid_cols, members
):
    step = pl.program_id(0)
    base = step * (tb * OBS_TILE)
    width = table_ref.shape[1]

    @pl.when(step == 0)
    def _():
        def build(c, carry):
            start = pl.multiple_of(c * 128, 128)
            values = window_ref[:, pl.ds(start, 128)]
            mean = jnp.mean(values, axis=0, keepdims=True)
            extra = aux_ref[:, pl.ds(start, 128)]
            first = lax.broadcasted_iota(jnp.int32, extra.shape, 0) == 0
            extra = jnp.where(first, extra - mean, extra)
            rows = jnp.concatenate(
                [values - mean, extra, jnp.zeros((width - members - 8, 128), jnp.float32)], axis=0
            )
            table_ref[pl.ds(start, 128), :] = rows.T
            return carry

        lax.fori_loop(0, table_ref.shape[0] // 128, build, 0)


    unroll = 32

    def gather(j, carry):
        first = pl.multiple_of(j * unroll, unroll)
        at = base + first
        for u in range(unroll):
            idx = picks_ref[at + u]
            buf_ref[pl.ds(first + u, 1), :] = table_ref[pl.ds(idx, 1), :]
        return carry

    lax.fori_loop(0, tb * OBS_TILE // unroll, gather, 0)
    row_first = meta_ref[0]
    for t in range(tb):
        n = step * tb + t
        tile_row = jnp.full((1, OBS_TILE), row_first + n // tile_cols, jnp.int32).astype(jnp.float32)
        tile_start = jnp.full((1, OBS_TILE), TILE_COLS * (n % tile_cols), jnp.int32).astype(
            jnp.float32
        )
        blk = buf_ref[pl.ds(t * OBS_TILE, OBS_TILE), :]
        blk_t = blk.T
        sig = blk_t[members + 1 : members + 2, :]
        orow = blk_t[members + 2 : members + 3, :]
        ocol = blk_t[members + 3 : members + 4, :]
        row_gap = orow - tile_row
        col_twice = 2.0 * ocol - 2.0 * tile_start - float(TILE_COLS - 1)
        col_twice = jnp.where(col_twice >= grid_cols, col_twice - 2.0 * grid_cols, col_twice)
        col_twice = jnp.where(col_twice < -grid_cols, col_twice + 2.0 * grid_cols, col_twice)
        col_gap = 0.5 * col_twice
        distance = row_gap * row_gap + col_gap * col_gap
        tapering = jnp.exp(-distance / (2.0 * LOC_RADIUS * LOC_RADIUS))
        weight = tapering / (sig * sig)
        lhs = blk_t[:members, :] * weight
        lhs_hi = lhs.astype(jnp.bfloat16)
        lhs_lo = (lhs - lhs_hi.astype(jnp.float32)).astype(jnp.bfloat16)
        rhs_hi = blk.astype(jnp.bfloat16)
        rhs_lo = (blk - rhs_hi.astype(jnp.float32)).astype(jnp.bfloat16)

        def product(x, y):
            return jnp.dot(x, y, preferred_element_type=jnp.float32)

        out_ref[t] = product(lhs_hi, rhs_hi) + (product(lhs_hi, rhs_lo) + product(lhs_lo, rhs_hi))


def gram_and_forcing(window, aux, picks, row_first, tile_cols, grid_cols):
    tile_count = picks.shape[0]
    tb = next(k for k in (16, 8, 1) if tile_count % k == 0)
    members, window_len = window.shape
    width = -(-(members + 8) // 128) * 128
    kernel = functools.partial(
        gram_kernel, tb=tb, tile_cols=tile_cols, grid_cols=grid_cols, members=members
    )
    meta = jnp.reshape(row_first, (1,)).astype(jnp.int32)
    return pl.pallas_call(
        kernel,
        grid_spec=pltpu.PrefetchScalarGridSpec(
            num_scalar_prefetch=2,
            grid=(tile_count // tb,),
            in_specs=[
                pl.BlockSpec((members, window_len), lambda s, p, m: (0, 0)),
                pl.BlockSpec(aux.shape, lambda s, p, m: (0, 0)),
            ],
            out_specs=pl.BlockSpec((tb, members, width), lambda s, p, m: (s, 0, 0)),
            scratch_shapes=[
                pltpu.VMEM((window_len, width), jnp.float32),
                pltpu.VMEM((tb * OBS_TILE, width), jnp.float32),
            ],
        ),
        out_shape=jax.ShapeDtypeStruct((tile_count, members, width), jnp.float32),
        compiler_params=pltpu.CompilerParams(dimension_semantics=("arbitrary",)),
    )(picks.reshape(-1), meta, window, aux)


def transform_of(moments, members):
    gram_matrix = moments[:, :, :members]
    forcing = moments[:, :, members]
    identity = jnp.eye(members, dtype=jnp.float32)
    system = gram_matrix + (members - 1.0) * identity
    frob_norm = jnp.sqrt(jnp.sum(system * system, axis=(1, 2)))
    iterate = system / frob_norm[:, None, None]
    factor = 1.5 * identity - 0.5 * iterate
    iterate = jnp.einsum("nij,njk->nik", iterate, factor, precision=lax.Precision.HIGH)
    inverse_root = factor
    for _ in range(1, NS_ITERS):
        factor = 1.5 * identity - 0.5 * jnp.einsum(
            "nij,njk->nik", inverse_root, iterate, precision=lax.Precision.HIGH
        )
        iterate = jnp.einsum("nij,njk->nik", iterate, factor, precision=lax.Precision.HIGH)
        inverse_root = jnp.einsum("nij,njk->nik", factor, inverse_root, precision=lax.Precision.HIGH)
    half_step = jnp.einsum("nkj,nj->nk", inverse_root, forcing, precision=highest)
    mean_weight = (
        jnp.einsum("nkj,nj->nk", inverse_root, half_step, precision=highest) / frob_norm[:, None]
    )
    return (
        jnp.sqrt(members - 1.0) * inverse_root / jnp.sqrt(frob_norm)[:, None, None]
        + mean_weight[:, :, None]
    )


def analysis_of(cells, transform):
    members, block_rows, block_cols = cells.shape
    tile_cells = cells.reshape(members, -1, TILE_COLS)
    centre_mean = jnp.mean(tile_cells, axis=0)
    spread = tile_cells - centre_mean
    analysis = centre_mean + jnp.einsum("jnt,njk->knt", spread, transform, precision=highest)
    return analysis.reshape(members, block_rows, block_cols)


def on_device(
    ensemble,
    spreading_number,
    zonal_transport_ratio,
    meridional_transport_ratio,
    ocean_mask,
    obs_loc,
    obs_value,
    obs_sigma,
    tile_obs,
):
    mem_dev, row_count, col_count = ensemble.shape
    liquid_cell_flags = ocean_mask.astype(jnp.float32)
    level_state_grid = forecast(
        ensemble,
        liquid_cell_flags,
        spreading_number,
        zonal_transport_ratio,
        meridional_transport_ratio,
    )
    space_index = lax.axis_index("space")
    member_index = lax.axis_index("member")
    obs_dev = obs_loc.shape[0] // lax.axis_size("space")
    flattened = level_state_grid.reshape(mem_dev, row_count * col_count)
    own_loc = lax.dynamic_slice_in_dim(obs_loc, space_index * obs_dev, obs_dev) - space_index * (
        row_count * col_count
    )
    own_obs = jnp.take(flattened, own_loc, axis=1)
    window = padded(gather_members(own_obs, "member"), (("space", 1),), obs_dev)
    window_len = window.shape[1]

    def window_of(values, fill):
        rim = jnp.full((obs_dev,), fill, values.dtype)
        return lax.dynamic_slice_in_dim(
            jnp.concatenate([rim, values, rim]), space_index * obs_dev, window_len
        )

    window_loc = window_of(obs_loc, 0)
    aux = jnp.concatenate(
        [
            window_of(obs_value, 0.0)[None],
            window_of(obs_sigma, 1.0)[None],
            (window_loc // col_count).astype(jnp.float32)[None],
            (window_loc % col_count).astype(jnp.float32)[None],
            jnp.zeros((4, window_len), jnp.float32),
        ],
        axis=0,
    )
    first_obs = (space_index - 1) * obs_dev
    member_count = lax.axis_size("member")
    block_rows = row_count // member_count
    cell_block = exchange(
        level_state_grid.reshape(mem_dev, member_count, block_rows, col_count).transpose(
            1, 0, 2, 3
        ),
        "member",
        0,
        mem_dev,
    )
    tile_picks = lax.dynamic_slice_in_dim(tile_obs, member_index * block_rows, block_rows, 0)
    local_picks = jnp.clip(tile_picks - first_obs, 0, window_len - 1)
    row_first = space_index * row_count + member_index * block_rows
    members = window.shape[0]
    tile_cols = col_count // TILE_COLS
    moments = gram_and_forcing(
        window,
        aux,
        local_picks.reshape(block_rows * tile_cols, -1),
        row_first,
        tile_cols,
        col_count,
    )
    split = tile_cols - (tile_cols * 3) // 8
    bounds = [(0, split), (split, tile_cols)] if 0 < split < tile_cols else [(0, tile_cols)]
    moments = moments.reshape(block_rows, tile_cols, members, moments.shape[-1])
    parts = []
    for first_col, last_col in bounds:
        picked = moments[:, first_col:last_col]
        transform = transform_of(
            picked.reshape(block_rows * (last_col - first_col), members, -1), members
        )
        lo, hi = first_col * TILE_COLS, last_col * TILE_COLS
        updated = analysis_of(cell_block[:, :, lo:hi], transform)
        parts.append(
            exchange(
                updated.reshape(member_count, mem_dev, block_rows, hi - lo),
                "member",
                1,
                block_rows,
            )
        )
    result = jnp.concatenate(parts, axis=2) if len(parts) > 1 else parts[0]
    return result


def solution(mesh):
    in_specs = (
        P("member", "space", None),
        P("space", None),
        P("space", None),
        P("space", None),
        P("space", None),
        P(),
        P(),
        P(),
        P("space", None, None),
    )
    out_specs = P("member", "space", None)

    return jax.shard_map(on_device, mesh=mesh, in_specs=in_specs, out_specs=out_specs, check_vma=False)
```

```python
import functools
import jax
import jax.numpy as jnp
from jax import lax
from jax.experimental import pallas as pl
from jax.experimental.pallas import tpu as pltpu
from jax.sharding import PartitionSpec as P


TILE_COLS = 128
OBS_TILE = 256
LOC_RADIUS = 96
NS_ITERS = 6


def padded(cells, sides, width):
    for axis, dim in sides:
        count = lax.axis_size(axis)
        ends = count - 1
        head = lax.slice_in_dim(cells, 0, width, axis=dim)
        tail = lax.slice_in_dim(cells, cells.shape[dim] - width, cells.shape[dim], axis=dim)
        cells = jnp.concatenate(
            [
                lax.ppermute(tail, axis, [(i, (i + 1) % count) for i in range(ends)]),
                cells,
                lax.ppermute(head, axis, [((i + 1) % count, i) for i in range(ends)]),
            ],
            axis=dim,
        )
    return cells


def exchange(blocks, axis, place_dim, place_len):
    count = lax.axis_size(axis)
    me = lax.axis_index(axis)
    shape = list(blocks.shape[1:])
    shape[place_dim] *= count
    result = jnp.zeros(shape, blocks.dtype)
    result = lax.dynamic_update_slice_in_dim(
        result, lax.dynamic_index_in_dim(blocks, me, keepdims=False), me * place_len, place_dim
    )
    for shift in range(1, count):
        partner = jnp.bitwise_xor(me, shift)
        sent = lax.dynamic_index_in_dim(blocks, partner, keepdims=False)
        got = lax.ppermute(sent, axis, [(i, i ^ shift) for i in range(count)])
        result = lax.dynamic_update_slice_in_dim(result, got, partner * place_len, place_dim)
    return result


def gather_members(block, axis):
    count = lax.axis_size(axis)
    me = lax.axis_index(axis)
    rows = block.shape[0]
    result = jnp.zeros((count * rows,) + block.shape[1:], block.dtype)
    result = lax.dynamic_update_slice_in_dim(result, block, me * rows, 0)
    for shift in range(1, count):
        partner = jnp.bitwise_xor(me, shift)
        got = lax.ppermute(block, axis, [(i, i ^ shift) for i in range(count)])
        result = lax.dynamic_update_slice_in_dim(result, got, partner * rows, 0)
    return result


def forecast_kernel(ens_ref, coef_ref, south_ref, north_ref, out_ref, state_ref, coef_ext_ref, step_ref):
    members, rows, cols = ens_ref.shape
    for k in range(4):
        plane, half = members + k // 2, k % 2
        coef_ext_ref[k, 0:1, :] = south_ref[plane, half : half + 1, :]
        coef_ext_ref[k, 1 : rows + 1, :] = coef_ref[k]
        coef_ext_ref[k, rows + 1 : rows + 2, :] = north_ref[plane, half : half + 1, :]

    def advance(centre, northern, southern, sea, spread, zonal, meridional):
        eastern = pltpu.roll(centre, cols - 1, 1)
        western = pltpu.roll(centre, 1, 1)
        laplace = northern + southern + eastern + western - 4.0 * centre
        advect = zonal * (eastern - western) * 0.5 + meridional * (northern - southern) * 0.5
        return sea * (centre + spread * laplace - advect)

    def member(m, carry):
        state_ref[0:2, :] = south_ref[m]
        state_ref[2 : rows + 2, :] = coef_ref[0] * ens_ref[m]
        state_ref[rows + 2 : rows + 4, :] = north_ref[m]
        step_ref[...] = advance(
            state_ref[1 : rows + 3, :],
            state_ref[2 : rows + 4, :],
            state_ref[0 : rows + 2, :],
            coef_ext_ref[0],
            coef_ext_ref[1],
            coef_ext_ref[2],
            coef_ext_ref[3],
        )
        out_ref[m] = advance(
            step_ref[1 : rows + 1, :],
            step_ref[2 : rows + 2, :],
            step_ref[0:rows, :],
            coef_ref[0],
            coef_ref[1],
            coef_ref[2],
            coef_ref[3],
        )
        return carry

    lax.fori_loop(0, members, member, 0)


def forecast(ensemble, sea, spreading_number, zonal_transport_ratio, meridional_transport_ratio):
    _, rows, cols = ensemble.shape
    coef = jnp.stack([sea, spreading_number, zonal_transport_ratio, meridional_transport_ratio])
    ends = lax.axis_size("space") - 1

    def edge(first, keep):
        state = coef[0, first : first + 2] * ensemble[:, first : first + 2]
        return jnp.concatenate([state, coef[:, keep].reshape(2, 2, cols)])

    south = lax.ppermute(edge(rows - 2, rows - 1), "space", [(i, i + 1) for i in range(ends)])
    north = lax.ppermute(edge(0, 0), "space", [(i + 1, i) for i in range(ends)])
    return pl.pallas_call(
        forecast_kernel,
        out_shape=jax.ShapeDtypeStruct(ensemble.shape, jnp.float32),
        in_specs=[pl.BlockSpec(memory_space=pltpu.VMEM)] * 4,
        out_specs=pl.BlockSpec(memory_space=pltpu.VMEM),
        scratch_shapes=[
            pltpu.VMEM((rows + 4, cols), jnp.float32),
            pltpu.VMEM((4, rows + 2, cols), jnp.float32),
            pltpu.VMEM((rows + 2, cols), jnp.float32),
        ],
    )(ensemble, coef, south, north)


def gram_kernel(
    picks_ref, meta_ref, window_ref, aux_ref, out_ref, table_ref, buf_ref, *, tb, tile_cols, grid_cols, members
):
    step = pl.program_id(0)
    base = step * (tb * OBS_TILE)
    width = table_ref.shape[1]

    @pl.when(step == 0)
    def _():
        def build(c, carry):
            start = pl.multiple_of(c * 128, 128)
            values = window_ref[:, pl.ds(start, 128)]
            mean = jnp.mean(values, axis=0, keepdims=True)
            extra = aux_ref[:, pl.ds(start, 128)]
            first = lax.broadcasted_iota(jnp.int32, extra.shape, 0) == 0
            extra = jnp.where(first, extra - mean, extra)
            rows = jnp.concatenate(
                [values - mean, extra, jnp.zeros((width - members - 8, 128), jnp.float32)], axis=0
            )
            table_ref[pl.ds(start, 128), :] = rows.T
            return carry

        lax.fori_loop(0, table_ref.shape[0] // 128, build, 0)


    unroll = 64

    def gather(j, carry):
        first = pl.multiple_of(j * unroll, unroll)
        at = base + first
        for u in range(unroll):
            idx = picks_ref[at + u]
            buf_ref[pl.ds(first + u, 1), :] = table_ref[pl.ds(idx, 1), :]
        return carry

    lax.fori_loop(0, tb * OBS_TILE // unroll, gather, 0)
    row_first = meta_ref[0]
    for t in range(tb):
        n = step * tb + t
        tile_row = jnp.full((1, OBS_TILE), row_first + n // tile_cols, jnp.int32).astype(jnp.float32)
        tile_start = jnp.full((1, OBS_TILE), TILE_COLS * (n % tile_cols), jnp.int32).astype(
            jnp.float32
        )
        blk = buf_ref[pl.ds(t * OBS_TILE, OBS_TILE), :]
        blk_t = blk.T
        sig = blk_t[members + 1 : members + 2, :]
        orow = blk_t[members + 2 : members + 3, :]
        ocol = blk_t[members + 3 : members + 4, :]
        row_gap = orow - tile_row
        col_twice = 2.0 * ocol - 2.0 * tile_start - float(TILE_COLS - 1)
        col_twice = jnp.where(col_twice >= grid_cols, col_twice - 2.0 * grid_cols, col_twice)
        col_twice = jnp.where(col_twice < -grid_cols, col_twice + 2.0 * grid_cols, col_twice)
        col_gap = 0.5 * col_twice
        distance = row_gap * row_gap + col_gap * col_gap
        tapering = jnp.exp(-distance / (2.0 * LOC_RADIUS * LOC_RADIUS))
        weight = tapering / (sig * sig)
        lhs = blk_t[:members, :] * weight
        lhs_hi = lhs.astype(jnp.bfloat16)
        lhs_lo = (lhs - lhs_hi.astype(jnp.float32)).astype(jnp.bfloat16)
        rhs_hi = blk.astype(jnp.bfloat16)
        rhs_lo = (blk - rhs_hi.astype(jnp.float32)).astype(jnp.bfloat16)

        def product(x, y):
            return jnp.dot(x, y, preferred_element_type=jnp.float32)

        out_ref[t] = product(lhs_hi, rhs_hi) + (product(lhs_hi, rhs_lo) + product(lhs_lo, rhs_hi))


def gram_and_forcing(window, aux, picks, row_first, tile_cols, grid_cols):
    tile_count = picks.shape[0]
    tb = next(k for k in (16, 8, 1) if tile_count % k == 0)
    members, window_len = window.shape
    width = -(-(members + 8) // 128) * 128
    kernel = functools.partial(
        gram_kernel, tb=tb, tile_cols=tile_cols, grid_cols=grid_cols, members=members
    )
    meta = jnp.reshape(row_first, (1,)).astype(jnp.int32)
    return pl.pallas_call(
        kernel,
        grid_spec=pltpu.PrefetchScalarGridSpec(
            num_scalar_prefetch=2,
            grid=(tile_count // tb,),
            in_specs=[
                pl.BlockSpec((members, window_len), lambda s, p, m: (0, 0)),
                pl.BlockSpec(aux.shape, lambda s, p, m: (0, 0)),
            ],
            out_specs=pl.BlockSpec((tb, members, width), lambda s, p, m: (s, 0, 0)),
            scratch_shapes=[
                pltpu.VMEM((window_len, width), jnp.float32),
                pltpu.VMEM((tb * OBS_TILE, width), jnp.float32),
            ],
        ),
        out_shape=jax.ShapeDtypeStruct((tile_count, members, width), jnp.float32),
        compiler_params=pltpu.CompilerParams(dimension_semantics=("arbitrary",)),
    )(picks.reshape(-1), meta, window, aux)


def transform_of(moments, members):
    gram_matrix = moments[:, :, :members]
    forcing = moments[:, :, members]
    identity = jnp.eye(members, dtype=jnp.float32)
    system = gram_matrix + (members - 1.0) * identity
    frob_norm = jnp.sqrt(jnp.sum(system * system, axis=(1, 2)))
    iterate = system / frob_norm[:, None, None]
    factor = 1.5 * identity - 0.5 * iterate
    iterate = jnp.einsum("nij,njk->nik", iterate, factor, precision=lax.Precision.HIGH)
    inverse_root = factor
    for _ in range(1, NS_ITERS):
        factor = 1.5 * identity - 0.5 * jnp.einsum(
            "nij,njk->nik", inverse_root, iterate, precision=lax.Precision.HIGH
        )
        iterate = jnp.einsum("nij,njk->nik", iterate, factor, precision=lax.Precision.HIGH)
        inverse_root = jnp.einsum("nij,njk->nik", factor, inverse_root, precision=lax.Precision.HIGH)
    half_step = jnp.einsum("nkj,nj->nk", inverse_root, forcing, precision=lax.Precision.HIGH)
    mean_weight = (
        jnp.einsum("nkj,nj->nk", inverse_root, half_step, precision=lax.Precision.HIGH) / frob_norm[:, None]
    )
    return (
        jnp.sqrt(members - 1.0) * inverse_root / jnp.sqrt(frob_norm)[:, None, None]
        + mean_weight[:, :, None]
    )


def analysis_of(cells, transform):
    members, block_rows, block_cols = cells.shape
    tile_cells = cells.reshape(members, -1, TILE_COLS)
    centre_mean = jnp.mean(tile_cells, axis=0)
    spread = tile_cells - centre_mean
    analysis = centre_mean + jnp.einsum("jnt,njk->knt", spread, transform, precision=lax.Precision.HIGH)
    return analysis.reshape(members, block_rows, block_cols)


def on_device(
    ensemble,
    spreading_number,
    zonal_transport_ratio,
    meridional_transport_ratio,
    ocean_mask,
    obs_loc,
    obs_value,
    obs_sigma,
    tile_obs,
):
    mem_dev, row_count, col_count = ensemble.shape
    liquid_cell_flags = ocean_mask.astype(jnp.float32)
    level_state_grid = forecast(
        ensemble,
        liquid_cell_flags,
        spreading_number,
        zonal_transport_ratio,
        meridional_transport_ratio,
    )
    space_index = lax.axis_index("space")
    member_index = lax.axis_index("member")
    obs_dev = obs_loc.shape[0] // lax.axis_size("space")
    flattened = level_state_grid.reshape(mem_dev, row_count * col_count)
    own_loc = lax.dynamic_slice_in_dim(obs_loc, space_index * obs_dev, obs_dev) - space_index * (
        row_count * col_count
    )
    own_obs = jnp.take(flattened, own_loc, axis=1)
    window = padded(gather_members(own_obs, "member"), (("space", 1),), obs_dev)
    window_len = window.shape[1]

    def window_of(values, fill):
        rim = jnp.full((obs_dev,), fill, values.dtype)
        return lax.dynamic_slice_in_dim(
            jnp.concatenate([rim, values, rim]), space_index * obs_dev, window_len
        )

    window_loc = window_of(obs_loc, 0)
    aux = jnp.concatenate(
        [
            window_of(obs_value, 0.0)[None],
            window_of(obs_sigma, 1.0)[None],
            (window_loc // col_count).astype(jnp.float32)[None],
            (window_loc % col_count).astype(jnp.float32)[None],
            jnp.zeros((4, window_len), jnp.float32),
        ],
        axis=0,
    )
    first_obs = (space_index - 1) * obs_dev
    member_count = lax.axis_size("member")
    block_rows = row_count // member_count
    cell_block = exchange(
        level_state_grid.reshape(mem_dev, member_count, block_rows, col_count).transpose(
            1, 0, 2, 3
        ),
        "member",
        0,
        mem_dev,
    )
    tile_picks = lax.dynamic_slice_in_dim(tile_obs, member_index * block_rows, block_rows, 0)
    local_picks = jnp.clip(tile_picks - first_obs, 0, window_len - 1)
    row_first = space_index * row_count + member_index * block_rows
    members = window.shape[0]
    tile_cols = col_count // TILE_COLS
    moments = gram_and_forcing(
        window,
        aux,
        local_picks.reshape(block_rows * tile_cols, -1),
        row_first,
        tile_cols,
        col_count,
    )
    halves = 2 if tile_cols % 2 == 0 else 1
    part_cols = tile_cols // halves
    moments = moments.reshape(block_rows, tile_cols, members, moments.shape[-1])
    parts = []
    for half in range(halves):
        picked = moments[:, half * part_cols : (half + 1) * part_cols]
        transform = transform_of(picked.reshape(block_rows * part_cols, members, -1), members)
        lo, hi = half * part_cols * TILE_COLS, (half + 1) * part_cols * TILE_COLS
        updated = analysis_of(cell_block[:, :, lo:hi], transform)
        parts.append(
            exchange(
                updated.reshape(member_count, mem_dev, block_rows, hi - lo),
                "member",
                1,
                block_rows,
            )
        )
    result = jnp.concatenate(parts, axis=2) if halves > 1 else parts[0]
    return result


def solution(mesh):
    in_specs = (
        P("member", "space", None),
        P("space", None),
        P("space", None),
        P("space", None),
        P("space", None),
        P(),
        P(),
        P(),
        P("space", None, None),
    )
    out_specs = P("member", "space", None)

    return jax.shard_map(on_device, mesh=mesh, in_specs=in_specs, out_specs=out_specs, check_vma=False)
```
